32 devices in a mesh: outer: 8 (over z, x), inner: 4 (over y, core).
Axes of the slice: x: 2, y: 2, z: 4, core: 2. Of those that a mesh axis runs over, the one named last changes fastest.
Arguments:
- query_rows: bfloat16 [4096, 4096], P(('outer', 'inner')), may hold values from -17 to 17
- key_matrix: bfloat16 [4096, 512], P(('outer', 'inner')), may hold values from -6 to 6
- value_matrix: bfloat16 [4096, 512], P(('outer', 'inner')), may hold values from -5 to 5
- unit_order: int32 [8], replicated, may hold values from 0 to 7, each once
- doc_lengths: int32 [8], replicated, may hold values from 1 to 1024, 4096 in all
Outputs:
- attended: bfloat16 [4096, 4096], P(('outer', 'inner'))
The draws below stay inside these ranges and needn't reach their ends.
All inputs are finite; a program needn't handle non-finite values.
Results may differ from the reference program's by a relative error of at most 0.0037.
Values may be sent and summed in bfloat16 or wider, within the bound.
No kernel may reach another device: no remote copies, remote signals or barrier semaphores. Data moves between devices by JAX's collectives and lax.ppermute only.
A program may use at most 64 MiB of HBM per device.

```python
import math
import jax
import jax.numpy as jnp
import numpy as np
from jax import lax

QUERY_HEADS = 32
KEY_VALUE_HEADS = 4
HEAD_SIZE = 128
UNIT_TOKENS = 512
PACKED_TOKENS = 4096
UNITS = 8
DOC_MOST = 1024
DOCS = 8


def joint_draw(key):
    key_start = jax.random.fold_in(key, 11)
    query_base = jax.random.fold_in(key, 12)
    final_keys = jnp.clip(jax.random.normal(key_start, (PACKED_TOKENS, KEY_VALUE_HEADS * HEAD_SIZE), jnp.float32), -4.0, 4.0)
    queries_final = jnp.clip(jax.random.normal(query_base, (PACKED_TOKENS, QUERY_HEADS * HEAD_SIZE), jnp.float32), -4.0, 4.0)
    return (queries_final, final_keys)


def draw_query_rows(key, part):
    return joint_draw(key)[0].astype(jnp.bfloat16)


def draw_key_matrix(key, part):
    return joint_draw(key)[1].astype(jnp.bfloat16)


def shard_levels(stream_key, shape, shards, low, top_value):
    def one(axis_at, shards_of):
        draws = jax.random.uniform(jax.random.fold_in(jax.random.fold_in(stream_key, 6), axis_at), (shards_of,), jnp.float32, low / len(shards), top_value / len(shards))
        return jnp.repeat(jnp.exp(draws), shape[axis_at] // shards_of).reshape((-1,) + (1,) * (len(shape) - axis_at - 1))

    loudness = one(*shards[0])
    for cut in shards[1:]:
        loudness = loudness * one(*cut)
    return loudness


def profile(number_of, total, bound, skew):
    loads = [(1 << 20) // math.isqrt(rank ** skew) + 1 for rank in range(2, number_of + 1)]
    surplus, holding = total - bound - (number_of - 1), [1] * (number_of - 1)
    while surplus > 0:
        movable = [i for i in range(number_of - 1) if holding[i] < bound]
        mass, budget = sum([loads[i] for i in movable]), surplus
        for i in movable:
            more = min(bound - holding[i], max(1, budget * loads[i] // mass), surplus)
            holding[i] = holding[i] + more
            surplus = surplus - more
    return np.array([bound] + holding)


def ragged_sizes(key, number_of, total, bound, lean):
    if number_of == 2:
        one = jax.random.randint(key, (), max(1, total - bound), min(bound, total - 1) + 1)
        return jnp.stack([one, total - one])
    lengths = jnp.asarray(profile(number_of, total, bound, lean), jnp.int32)
    couples = (number_of - 1) // 2
    donor, taker = lengths[1:1 + 2 * couples:2], lengths[2:2 + 2 * couples:2]
    slack = jnp.minimum(donor - 1, bound - taker)
    shifted = jax.random.randint(jax.random.fold_in(key, 1), (couples,), 0, 1 << 20) % (slack + 1)
    lengths = lengths.at[1:1 + 2 * couples:2].set(donor - shifted).at[2:2 + 2 * couples:2].set(taker + shifted)
    return lengths[jax.random.permutation(jax.random.fold_in(key, 2), number_of)]


def noise(own_key, dims, scale, bound, split=(), kind=jnp.bfloat16):
    drawn = jax.random.normal(own_key, dims, jnp.float32) * scale
    if len(split) > 0:
        drawn = shard_levels(own_key, dims, split, -0.22, 0.18) * drawn
    return jnp.clip(drawn, min=-bound, max=bound).astype(kind)


def setup_inputs(seed: int = 0) -> dict:
    splits = jax.random.split(jax.random.key(seed), 6)
    query_rows = draw_query_rows(jax.random.fold_in(splits[5], 71), 0)
    key_matrix = draw_key_matrix(jax.random.fold_in(splits[5], 71), 0)
    value_matrix = noise(splits[2], (PACKED_TOKENS, KEY_VALUE_HEADS * HEAD_SIZE), 1.0, 5.0, ((0, 32),))
    unit_order = jax.random.permutation(splits[3], UNITS).astype(jnp.int32)
    doc_lengths = ragged_sizes(splits[4], DOCS, PACKED_TOKENS, DOC_MOST, 2).astype(jnp.int32)
    return dict(query_rows=query_rows, key_matrix=key_matrix, value_matrix=value_matrix, unit_order=unit_order, doc_lengths=doc_lengths)


NEG_FILL = -1.0e30


def reference(query_rows, key_matrix, value_matrix, unit_order, doc_lengths):
    unit_count = PACKED_TOKENS // UNIT_TOKENS
    extent = -(-DOC_MOST // UNIT_TOKENS)
    group_share = QUERY_HEADS // KEY_VALUE_HEADS
    view_window = (extent + 1) * UNIT_TOKENS

    def position_lookup(score_matrix):
        shaped = score_matrix.reshape(unit_count, UNIT_TOKENS, score_matrix.shape[1])
        return jnp.zeros_like(shaped).at[unit_order].set(shaped)

    queries_sorted = position_lookup(query_rows)
    pad_amount = jnp.zeros((extent * UNIT_TOKENS, KEY_VALUE_HEADS * HEAD_SIZE), jnp.bfloat16)
    keys_padded = jnp.concatenate([pad_amount, position_lookup(key_matrix).reshape(PACKED_TOKENS, KEY_VALUE_HEADS * HEAD_SIZE)], 0)
    values_padded = jnp.concatenate([pad_amount, position_lookup(value_matrix).reshape(PACKED_TOKENS, KEY_VALUE_HEADS * HEAD_SIZE)], 0)
    doc_ends = jnp.cumsum(doc_lengths).astype(jnp.int32)
    positions = jnp.arange(PACKED_TOKENS, dtype=jnp.int32)
    doc_ids = jnp.sum((doc_ends[None, :] <= positions[:, None]).astype(jnp.int32), axis=1).astype(jnp.int32)
    padded_docs = jnp.concatenate([jnp.full((extent * UNIT_TOKENS,), -1, jnp.int32), doc_ids])
    padded_pos = jnp.arange(-extent * UNIT_TOKENS, PACKED_TOKENS, dtype=jnp.int32)

    def one_block(block_slice):
        start_offset = (block_slice * UNIT_TOKENS).astype(jnp.int32)
        query_piece = queries_sorted[block_slice].astype(jnp.float32).reshape(UNIT_TOKENS, KEY_VALUE_HEADS, group_share, HEAD_SIZE)
        key_piece = lax.dynamic_slice_in_dim(keys_padded, start_offset, view_window, 0).astype(jnp.float32).reshape(view_window, KEY_VALUE_HEADS, HEAD_SIZE)
        value_piece = lax.dynamic_slice_in_dim(values_padded, start_offset, view_window, 0).astype(jnp.float32).reshape(view_window, KEY_VALUE_HEADS, HEAD_SIZE)
        query_docs = lax.dynamic_slice_in_dim(doc_ids, start_offset, UNIT_TOKENS, 0)
        query_pos = start_offset + jnp.arange(UNIT_TOKENS, dtype=jnp.int32)
        key_docs = lax.dynamic_slice_in_dim(padded_docs, start_offset, view_window, 0)
        key_pos = lax.dynamic_slice_in_dim(padded_pos, start_offset, view_window, 0)
        allowed = (query_docs[:, None] == key_docs[None, :]) & (key_pos[None, :] <= query_pos[:, None])
        scores = jnp.einsum("qhgd,khd->hgqk", query_piece, key_piece) * (HEAD_SIZE ** -0.5)
        scores = jnp.where(allowed, scores, NEG_FILL)
        highest = jnp.max(scores, axis=3, keepdims=True)
        weights = jnp.where(allowed, jnp.exp(scores - highest), 0.0)
        totals = jnp.sum(weights, axis=3)
        rounded = lax.optimization_barrier(weights.astype(jnp.bfloat16)).astype(jnp.float32)
        mixed = jnp.einsum("hgqk,khd->qhgd", rounded, value_piece)
        result = mixed / jnp.transpose(totals, (2, 0, 1))[..., None]
        return result.reshape(UNIT_TOKENS, QUERY_HEADS * HEAD_SIZE).astype(jnp.bfloat16)

    blocks = lax.map(one_block, jnp.arange(unit_count, dtype=jnp.int32))
    return blocks[unit_order].reshape(PACKED_TOKENS, QUERY_HEADS * HEAD_SIZE)
```

```python
import jax
import jax.numpy as jnp
from jax import lax
from jax.sharding import PartitionSpec as P

QUERY_HEADS = 32
KEY_VALUE_HEADS = 4
HEAD_SIZE = 128
UNIT_TOKENS = 512


NEG_FILL = -1e30


def tile_update(running, query_piece, key_piece, value_piece, query_pos, query_start, key_pos):
    old_max, old_total, old_accum = running
    tile_rows, heads_here, _ = query_piece.shape
    allowed = (key_pos[None, :] >= query_start[:, None]) & (key_pos[None, :] <= query_pos[:, None])
    scores = jnp.einsum(
        "qhd,kd->hqk", query_piece, key_piece, preferred_element_type=jnp.float32
    ) * HEAD_SIZE ** (-0.5)
    scores = jnp.where(allowed[None], scores, NEG_FILL)
    new_max = jnp.maximum(old_max, jnp.max(scores, axis=2))
    weights = jnp.where(allowed[None], jnp.exp(scores - new_max[:, :, None]), 0.0)
    factor = jnp.exp(old_max - new_max)
    new_total = old_total * factor + jnp.sum(weights, axis=2)
    update = jnp.einsum(
        "hqk,kd->qhd",
        weights.astype(jnp.bfloat16),
        value_piece,
        preferred_element_type=jnp.float32,
    )
    new_accum = old_accum * factor.T[:, :, None] + update
    return (new_max, new_total, new_accum)


def body(query_rows, key_matrix, value_matrix, unit_order, doc_lengths):
    inner_steps = lax.axis_size("inner")
    token_total = query_rows.shape[0]
    group_rows = inner_steps * token_total
    heads_here = QUERY_HEADS // inner_steps
    head_copies = inner_steps // KEY_VALUE_HEADS
    local_queries = lax.all_to_all(query_rows, "inner", split_axis=1, concat_axis=0, tiled=True)

    def widened_heads(score_matrix):
        return jnp.repeat(
            score_matrix.reshape(token_total, KEY_VALUE_HEADS, HEAD_SIZE), head_copies, axis=1
        ).reshape(token_total, inner_steps * HEAD_SIZE)

    own_keys = lax.all_to_all(
        widened_heads(key_matrix), "inner", split_axis=1, concat_axis=0, tiled=True
    )
    own_values = lax.all_to_all(
        widened_heads(value_matrix), "inner", split_axis=1, concat_axis=0, tiled=True
    )
    all_keys = lax.all_gather(own_keys, "outer", axis=0, tiled=True)
    all_values = lax.all_gather(own_values, "outer", axis=0, tiled=True)

    unit_count = unit_order.shape[0]
    inverse = jnp.zeros((unit_count,), jnp.int32).at[unit_order].set(
        jnp.arange(unit_count, dtype=jnp.int32)
    )
    doc_ends = jnp.cumsum(doc_lengths).astype(jnp.int32)
    group_units = group_rows // UNIT_TOKENS
    group_begin = lax.axis_index("outer") * group_units
    offsets = jnp.arange(UNIT_TOKENS, dtype=jnp.int32)
    shaped_queries = local_queries.reshape(group_rows, heads_here, HEAD_SIZE)

    outputs = []
    for query_unit in range(group_units):
        position_unit = unit_order[group_begin + query_unit]
        query_pos = position_unit * UNIT_TOKENS + offsets
        query_start = jnp.max(
            jnp.where(doc_ends[None, :] <= query_pos[:, None], doc_ends[None, :], 0), axis=1
        )
        first_unit = query_start[0] // UNIT_TOKENS
        query_piece = shaped_queries[query_unit * UNIT_TOKENS : (query_unit + 1) * UNIT_TOKENS]

        def visit(step, carried):
            key_unit = position_unit - step
            key_row = inverse[key_unit] * UNIT_TOKENS
            key_piece = lax.dynamic_slice_in_dim(all_keys, key_row, UNIT_TOKENS, 0)
            value_piece = lax.dynamic_slice_in_dim(all_values, key_row, UNIT_TOKENS, 0)
            key_pos = key_unit * UNIT_TOKENS + offsets
            return tile_update(
                carried, query_piece, key_piece, value_piece, query_pos, query_start, key_pos
            )

        running = (
            jnp.full((heads_here, UNIT_TOKENS), NEG_FILL, jnp.float32),
            jnp.zeros((heads_here, UNIT_TOKENS), jnp.float32),
            jnp.zeros((UNIT_TOKENS, heads_here, HEAD_SIZE), jnp.float32),
        )
        _, totals, accumulated = lax.fori_loop(
            0, position_unit - first_unit + 1, visit, running
        )
        outputs.append(
            (accumulated / totals.T[:, :, None])
            .reshape(UNIT_TOKENS, heads_here * HEAD_SIZE)
            .astype(jnp.bfloat16)
        )
    normalized = jnp.concatenate(outputs, axis=0) if len(outputs) > 1 else outputs[0]
    return lax.all_to_all(normalized, "inner", split_axis=0, concat_axis=1, tiled=True)


def solution(mesh):
    placed = (
        P(("outer", "inner"), None),
        P(("outer", "inner"), None),
        P(("outer", "inner"), None),
        P(),
        P(),
    )
    return jax.shard_map(
        body, mesh=mesh, in_specs=placed, out_specs=P(("outer", "inner"), None), check_vma=False
    )
```

```python
import jax
import jax.numpy as jnp
from jax import lax
from jax.sharding import PartitionSpec as P

QUERY_HEADS = 32
KEY_VALUE_HEADS = 4
HEAD_SIZE = 128
UNIT_TOKENS = 512


NEG_FILL = -1e30


def tile_update(running, query_piece, key_piece, value_piece, query_pos, query_start, key_pos):
    old_max, old_total, old_accum = running
    tile_rows, heads_here, _ = query_piece.shape
    allowed = (key_pos[None, :] >= query_start[:, None]) & (key_pos[None, :] <= query_pos[:, None])
    scores = jnp.einsum(
        "qhd,kd->hqk", query_piece, key_piece, preferred_element_type=jnp.float32
    ) * HEAD_SIZE ** (-0.5)
    scores = jnp.where(allowed[None], scores, NEG_FILL)
    new_max = jnp.maximum(old_max, jnp.max(scores, axis=2))
    weights = jnp.where(allowed[None], jnp.exp(scores - new_max[:, :, None]), 0.0)
    factor = jnp.exp(old_max - new_max)
    new_total = old_total * factor + jnp.sum(weights, axis=2)
    update = jnp.einsum(
        "hqk,kd->qhd",
        weights.astype(jnp.bfloat16),
        value_piece,
        preferred_element_type=jnp.float32,
    )
    new_accum = old_accum * factor.T[:, :, None] + update
    return (new_max, new_total, new_accum)


def body(query_rows, key_matrix, value_matrix, unit_order, doc_lengths):
    inner_steps = lax.axis_size("inner")
    token_total = query_rows.shape[0]
    group_rows = inner_steps * token_total
    heads_here = QUERY_HEADS // inner_steps
    head_copies = inner_steps // KEY_VALUE_HEADS
    query_width = heads_here * HEAD_SIZE

    def widened_heads(score_matrix):
        return jnp.repeat(
            score_matrix.reshape(token_total, KEY_VALUE_HEADS, HEAD_SIZE), head_copies, axis=1
        )

    joined = jnp.concatenate(
        [
            query_rows.reshape(token_total, inner_steps, query_width),
            widened_heads(key_matrix),
            widened_heads(value_matrix),
        ],
        axis=2,
    )
    gathered = lax.all_to_all(joined, "inner", split_axis=1, concat_axis=0, tiled=True)
    gathered = gathered.reshape(group_rows, query_width + 2 * HEAD_SIZE)
    local_queries = gathered[:, :query_width]
    own_pairs = gathered[:, query_width:]
    outer_count = lax.axis_size("outer")
    outer_index = lax.axis_index("outer")
    received = [own_pairs]
    for distance in range(1, outer_count):
        route = [(i, (i + distance) % outer_count) for i in range(outer_count)]
        received.append(lax.ppermute(own_pairs, "outer", route))
    all_pairs = jnp.stack(received)

    unit_count = unit_order.shape[0]
    inverse = jnp.zeros((unit_count,), jnp.int32).at[unit_order].set(
        jnp.arange(unit_count, dtype=jnp.int32)
    )
    doc_ends = jnp.cumsum(doc_lengths).astype(jnp.int32)
    group_units = group_rows // UNIT_TOKENS
    group_begin = outer_index * group_units
    offsets = jnp.arange(UNIT_TOKENS, dtype=jnp.int32)
    shaped_queries = local_queries.reshape(group_rows, heads_here, HEAD_SIZE)

    outputs = []
    for query_unit in range(group_units):
        position_unit = unit_order[group_begin + query_unit]
        query_pos = position_unit * UNIT_TOKENS + offsets
        query_start = jnp.max(
            jnp.where(doc_ends[None, :] <= query_pos[:, None], doc_ends[None, :], 0), axis=1
        )
        first_unit = query_start[0] // UNIT_TOKENS
        query_piece = shaped_queries[query_unit * UNIT_TOKENS : (query_unit + 1) * UNIT_TOKENS]

        def visit(step, carried):
            key_unit = position_unit - step
            key_row_unit = inverse[key_unit]
            source = (outer_index - key_row_unit // group_units) % outer_count
            key_row = (key_row_unit % group_units) * UNIT_TOKENS
            pair_piece = lax.dynamic_slice(
                all_pairs, (source, key_row, 0), (1, UNIT_TOKENS, 2 * HEAD_SIZE)
            )[0]
            key_piece = pair_piece[:, :HEAD_SIZE]
            value_piece = pair_piece[:, HEAD_SIZE:]
            key_pos = key_unit * UNIT_TOKENS + offsets
            return tile_update(
                carried, query_piece, key_piece, value_piece, query_pos, query_start, key_pos
            )

        running = (
            jnp.full((heads_here, UNIT_TOKENS), NEG_FILL, jnp.float32),
            jnp.zeros((heads_here, UNIT_TOKENS), jnp.float32),
            jnp.zeros((UNIT_TOKENS, heads_here, HEAD_SIZE), jnp.float32),
        )
        _, totals, accumulated = lax.fori_loop(
            0, position_unit - first_unit + 1, visit, running
        )
        outputs.append(
            (accumulated / totals.T[:, :, None])
            .reshape(UNIT_TOKENS, heads_here * HEAD_SIZE)
            .astype(jnp.bfloat16)
        )
    normalized = jnp.concatenate(outputs, axis=0) if len(outputs) > 1 else outputs[0]
    return lax.all_to_all(normalized, "inner", split_axis=0, concat_axis=1, tiled=True)


def solution(mesh):
    placed = (
        P(("outer", "inner"), None),
        P(("outer", "inner"), None),
        P(("outer", "inner"), None),
        P(),
        P(),
    )
    return jax.shard_map(
        body, mesh=mesh, in_specs=placed, out_specs=P(("outer", "inner"), None), check_vma=False
    )
```

```python
import jax
import jax.numpy as jnp
from jax import lax
from jax.sharding import PartitionSpec as P

QUERY_HEADS = 32
KEY_VALUE_HEADS = 4
HEAD_SIZE = 128
UNIT_TOKENS = 512


NEG_FILL = -1e30


def tile_update(running, query_piece, key_piece, value_piece, query_pos, query_start, key_pos):
    old_max, old_total, old_accum = running
    tile_rows, heads_here, _ = query_piece.shape
    allowed = (key_pos[None, :] >= query_start[:, None]) & (key_pos[None, :] <= query_pos[:, None])
    scores = jnp.einsum(
        "qhd,kd->hqk", query_piece, key_piece, preferred_element_type=jnp.float32
    ) * HEAD_SIZE ** (-0.5)
    scores = jnp.where(allowed[None], scores, NEG_FILL)
    new_max = jnp.maximum(old_max, jnp.max(scores, axis=2))
    weights = jnp.where(allowed[None], jnp.exp(scores - new_max[:, :, None]), 0.0)
    factor = jnp.exp(old_max - new_max)
    new_total = old_total * factor + jnp.sum(weights, axis=2)
    update = jnp.einsum(
        "hqk,kd->qhd",
        weights.astype(jnp.bfloat16),
        value_piece,
        preferred_element_type=jnp.float32,
    )
    new_accum = old_accum * factor.T[:, :, None] + update
    return (new_max, new_total, new_accum)


def body(query_rows, key_matrix, value_matrix, unit_order, doc_lengths):
    inner_steps = lax.axis_size("inner")
    token_total = query_rows.shape[0]
    group_rows = inner_steps * token_total
    heads_here = QUERY_HEADS // inner_steps
    head_copies = inner_steps // KEY_VALUE_HEADS
    query_width = heads_here * HEAD_SIZE

    def widened_heads(score_matrix):
        return jnp.repeat(
            score_matrix.reshape(token_total, KEY_VALUE_HEADS, HEAD_SIZE), head_copies, axis=1
        )

    pairs = jnp.concatenate([widened_heads(key_matrix), widened_heads(value_matrix)], axis=2)
    own_pairs = lax.all_to_all(pairs, "inner", split_axis=1, concat_axis=0, tiled=True)
    own_pairs = own_pairs.reshape(group_rows, 2 * HEAD_SIZE)
    outer_count = lax.axis_size("outer")
    outer_index = lax.axis_index("outer")
    received = [own_pairs]
    for distance in range(1, outer_count):
        route = [(i, (i + distance) % outer_count) for i in range(outer_count)]
        received.append(lax.ppermute(own_pairs, "outer", route))
    local_queries = lax.all_to_all(query_rows, "inner", split_axis=1, concat_axis=0, tiled=True)

    unit_count = unit_order.shape[0]
    inverse = jnp.zeros((unit_count,), jnp.int32).at[unit_order].set(
        jnp.arange(unit_count, dtype=jnp.int32)
    )
    doc_ends = jnp.cumsum(doc_lengths).astype(jnp.int32)
    group_units = group_rows // UNIT_TOKENS
    group_begin = outer_index * group_units
    offsets = jnp.arange(UNIT_TOKENS, dtype=jnp.int32)
    shaped_queries = local_queries.reshape(group_rows, heads_here, HEAD_SIZE)

    outputs = []
    for query_unit in range(group_units):
        position_unit = unit_order[group_begin + query_unit]
        query_pos = position_unit * UNIT_TOKENS + offsets
        query_start = jnp.max(
            jnp.where(doc_ends[None, :] <= query_pos[:, None], doc_ends[None, :], 0), axis=1
        )
        first_unit = query_start[0] // UNIT_TOKENS
        query_piece = shaped_queries[query_unit * UNIT_TOKENS : (query_unit + 1) * UNIT_TOKENS]

        def tile_at(carried, step, pair_piece):
            key_unit = position_unit - step
            key_pos = key_unit * UNIT_TOKENS + offsets
            return tile_update(
                carried,
                query_piece,
                pair_piece[:, :HEAD_SIZE],
                pair_piece[:, HEAD_SIZE:],
                query_pos,
                query_start,
                key_pos,
            )

        def visit(step, carried):
            key_row_unit = inverse[position_unit - step]
            source = (outer_index - key_row_unit // group_units) % outer_count
            key_row = (key_row_unit % group_units) * UNIT_TOKENS
            pair_piece = lax.switch(
                source,
                [
                    (lambda row, block=block: lax.dynamic_slice_in_dim(block, row, UNIT_TOKENS, 0))
                    for block in received
                ],
                key_row,
            )
            return tile_at(carried, step, pair_piece)

        running = (
            jnp.full((heads_here, UNIT_TOKENS), NEG_FILL, jnp.float32),
            jnp.zeros((heads_here, UNIT_TOKENS), jnp.float32),
            jnp.zeros((UNIT_TOKENS, heads_here, HEAD_SIZE), jnp.float32),
        )
        own_row = query_unit * UNIT_TOKENS
        running = tile_at(running, 0, own_pairs[own_row : own_row + UNIT_TOKENS])
        _, totals, accumulated = lax.fori_loop(
            1, position_unit - first_unit + 1, visit, running
        )
        outputs.append(
            (accumulated / totals.T[:, :, None])
            .reshape(UNIT_TOKENS, heads_here * HEAD_SIZE)
            .astype(jnp.bfloat16)
        )
    normalized = jnp.concatenate(outputs, axis=0) if len(outputs) > 1 else outputs[0]
    return lax.all_to_all(normalized, "inner", split_axis=0, concat_axis=1, tiled=True)


def solution(mesh):
    placed = (
        P(("outer", "inner"), None),
        P(("outer", "inner"), None),
        P(("outer", "inner"), None),
        P(),
        P(),
    )
    return jax.shard_map(
        body, mesh=mesh, in_specs=placed, out_specs=P(("outer", "inner"), None), check_vma=False
    )
```

```python
import jax
import jax.numpy as jnp
from jax import lax
from jax.sharding import PartitionSpec as P

QUERY_HEADS = 32
KEY_VALUE_HEADS = 4
HEAD_SIZE = 128
UNIT_TOKENS = 512


NEG_FILL = -1e30


def tile_update(running, query_piece, key_piece, value_piece, query_pos, query_start, key_pos):
    old_max, old_total, old_accum = running
    tile_rows, heads_here, _ = query_piece.shape
    allowed = (key_pos[None, :] >= query_start[:, None]) & (key_pos[None, :] <= query_pos[:, None])
    scores = jnp.einsum(
        "qhd,kd->hqk", query_piece, key_piece, preferred_element_type=jnp.float32
    ) * HEAD_SIZE ** (-0.5)
    scores = jnp.where(allowed[None], scores, NEG_FILL)
    new_max = jnp.maximum(old_max, jnp.max(scores, axis=2))
    weights = jnp.where(allowed[None], jnp.exp(scores - new_max[:, :, None]), 0.0)
    factor = jnp.exp(old_max - new_max)
    new_total = old_total * factor + jnp.sum(weights, axis=2)
    update = jnp.einsum(
        "hqk,kd->qhd",
        weights.astype(jnp.bfloat16),
        value_piece,
        preferred_element_type=jnp.float32,
    )
    new_accum = old_accum * factor.T[:, :, None] + update
    return (new_max, new_total, new_accum)


def body(query_rows, key_matrix, value_matrix, unit_order, doc_lengths):
    inner_steps = lax.axis_size("inner")
    token_total = query_rows.shape[0]
    group_rows = inner_steps * token_total
    heads_here = QUERY_HEADS // inner_steps
    head_copies = inner_steps // KEY_VALUE_HEADS
    query_width = heads_here * HEAD_SIZE

    def widened_heads(score_matrix):
        return jnp.repeat(
            score_matrix.reshape(token_total, KEY_VALUE_HEADS, HEAD_SIZE), head_copies, axis=1
        )

    pairs = jnp.concatenate([widened_heads(key_matrix), widened_heads(value_matrix)], axis=2)
    own_pairs = lax.all_to_all(pairs, "inner", split_axis=1, concat_axis=0, tiled=True)
    own_pairs = own_pairs.reshape(group_rows, 2 * HEAD_SIZE)
    outer_count = lax.axis_size("outer")
    outer_index = lax.axis_index("outer")
    received = [own_pairs]
    for distance in range(1, outer_count):
        route = [(i, (i + distance) % outer_count) for i in range(outer_count)]
        received.append(lax.ppermute(own_pairs, "outer", route))
    local_queries = lax.all_to_all(query_rows, "inner", split_axis=1, concat_axis=0, tiled=True)

    unit_count = unit_order.shape[0]
    unit_ids = jnp.arange(unit_count, dtype=jnp.int32)
    inverse = jnp.sum(
        jnp.where(unit_order[None, :] == unit_ids[:, None], unit_ids[None, :], 0), axis=1
    )
    doc_count = doc_lengths.shape[0]
    doc_ids = jnp.arange(doc_count, dtype=jnp.int32)
    doc_ends = jnp.sum(
        jnp.where(doc_ids[None, :] <= doc_ids[:, None], doc_lengths[None, :], 0), axis=1
    )
    group_units = group_rows // UNIT_TOKENS
    group_begin = outer_index * group_units
    offsets = jnp.arange(UNIT_TOKENS, dtype=jnp.int32)
    shaped_queries = local_queries.reshape(group_rows, heads_here, HEAD_SIZE)

    outputs = []
    for query_unit in range(group_units):
        position_unit = unit_order[group_begin + query_unit]
        query_pos = position_unit * UNIT_TOKENS + offsets
        query_start = jnp.max(
            jnp.where(doc_ends[None, :] <= query_pos[:, None], doc_ends[None, :], 0), axis=1
        )
        first_unit = query_start[0] // UNIT_TOKENS
        query_piece = shaped_queries[query_unit * UNIT_TOKENS : (query_unit + 1) * UNIT_TOKENS]

        def tile_at(carried, key_unit, pair_piece):
            key_pos = key_unit * UNIT_TOKENS + offsets
            return tile_update(
                carried,
                query_piece,
                pair_piece[:, :HEAD_SIZE],
                pair_piece[:, HEAD_SIZE:],
                query_pos,
                query_start,
                key_pos,
            )

        running = (
            jnp.full((heads_here, UNIT_TOKENS), NEG_FILL, jnp.float32),
            jnp.zeros((heads_here, UNIT_TOKENS), jnp.float32),
            jnp.zeros((UNIT_TOKENS, heads_here, HEAD_SIZE), jnp.float32),
        )
        own_row = query_unit * UNIT_TOKENS
        running = tile_at(running, position_unit, own_pairs[own_row : own_row + UNIT_TOKENS])

        if group_units == 1:
            for distance in range(1, outer_count):
                key_unit = unit_order[(outer_index - distance) % outer_count]
                needed = (key_unit >= first_unit) & (key_unit < position_unit)
                running = lax.cond(
                    needed,
                    lambda carried, key_unit=key_unit, block=received[distance]: tile_at(
                        carried, key_unit, block
                    ),
                    lambda carried: carried,
                    running,
                )
        else:

            def visit(step, carried):
                key_row_unit = inverse[position_unit - step]
                source = (outer_index - key_row_unit // group_units) % outer_count
                key_row = (key_row_unit % group_units) * UNIT_TOKENS
                pair_piece = lax.switch(
                    source,
                    [
                        (
                            lambda row, block=block: lax.dynamic_slice_in_dim(
                                block, row, UNIT_TOKENS, 0
                            )
                        )
                        for block in received
                    ],
                    key_row,
                )
                return tile_at(carried, position_unit - step, pair_piece)

            running = lax.fori_loop(1, position_unit - first_unit + 1, visit, running)
        _, totals, accumulated = running
        outputs.append(
            (accumulated / totals.T[:, :, None])
            .reshape(UNIT_TOKENS, heads_here * HEAD_SIZE)
            .astype(jnp.bfloat16)
        )
    normalized = jnp.concatenate(outputs, axis=0) if len(outputs) > 1 else outputs[0]
    return lax.all_to_all(normalized, "inner", split_axis=0, concat_axis=1, tiled=True)


def solution(mesh):
    placed = (
        P(("outer", "inner"), None),
        P(("outer", "inner"), None),
        P(("outer", "inner"), None),
        P(),
        P(),
    )
    return jax.shard_map(
        body, mesh=mesh, in_specs=placed, out_specs=P(("outer", "inner"), None), check_vma=False
    )
```

```python
import jax
import jax.numpy as jnp
from jax import lax
from jax.sharding import PartitionSpec as P

QUERY_HEADS = 32
KEY_VALUE_HEADS = 4
HEAD_SIZE = 128
UNIT_TOKENS = 512


NEG_FILL = -1e30


def tile_update(running, query_piece, key_piece, value_piece, query_pos, query_start, key_pos):
    old_max, old_total, old_accum = running
    tile_rows, heads_here, _ = query_piece.shape
    allowed = (key_pos[None, :] >= query_start[:, None]) & (key_pos[None, :] <= query_pos[:, None])
    scores = jnp.einsum(
        "qhd,kd->hqk", query_piece, key_piece, preferred_element_type=jnp.float32
    ) * HEAD_SIZE ** (-0.5)
    scores = jnp.where(allowed[None], scores, NEG_FILL)
    new_max = jnp.maximum(old_max, jnp.max(scores, axis=2))
    weights = jnp.where(allowed[None], jnp.exp(scores - new_max[:, :, None]), 0.0)
    factor = jnp.exp(old_max - new_max)
    new_total = old_total * factor + jnp.sum(weights, axis=2)
    update = jnp.einsum(
        "hqk,kd->qhd",
        weights.astype(jnp.bfloat16),
        value_piece,
        preferred_element_type=jnp.float32,
    )
    new_accum = old_accum * factor.T[:, :, None] + update
    return (new_max, new_total, new_accum)


def body(query_rows, key_matrix, value_matrix, unit_order, doc_lengths):
    inner_steps = lax.axis_size("inner")
    token_total = query_rows.shape[0]
    group_rows = inner_steps * token_total
    heads_here = QUERY_HEADS // inner_steps
    head_copies = inner_steps // KEY_VALUE_HEADS
    query_width = heads_here * HEAD_SIZE

    def widened_heads(score_matrix):
        return jnp.repeat(
            score_matrix.reshape(token_total, KEY_VALUE_HEADS, HEAD_SIZE), head_copies, axis=1
        )

    outer_count = lax.axis_size("outer")
    outer_index = lax.axis_index("outer")
    pairs = jnp.concatenate([widened_heads(key_matrix), widened_heads(value_matrix)], axis=2)
    spread = jnp.broadcast_to(
        jnp.transpose(pairs, (1, 0, 2))[None],
        (outer_count, inner_steps, token_total, 2 * HEAD_SIZE),
    ).reshape(outer_count * inner_steps, token_total, 2 * HEAD_SIZE)
    everyone = lax.all_to_all(spread, ("outer", "inner"), split_axis=0, concat_axis=0, tiled=True)
    everyone = everyone.reshape(outer_count, group_rows, 2 * HEAD_SIZE)
    own_pairs = lax.dynamic_index_in_dim(everyone, outer_index, 0, keepdims=False)
    local_queries = lax.all_to_all(query_rows, "inner", split_axis=1, concat_axis=0, tiled=True)

    unit_count = unit_order.shape[0]
    inverse = jnp.zeros((unit_count,), jnp.int32).at[unit_order].set(
        jnp.arange(unit_count, dtype=jnp.int32)
    )
    doc_ends = jnp.cumsum(doc_lengths).astype(jnp.int32)
    group_units = group_rows // UNIT_TOKENS
    group_begin = outer_index * group_units
    offsets = jnp.arange(UNIT_TOKENS, dtype=jnp.int32)
    shaped_queries = local_queries.reshape(group_rows, heads_here, HEAD_SIZE)

    outputs = []
    for query_unit in range(group_units):
        position_unit = unit_order[group_begin + query_unit]
        query_pos = position_unit * UNIT_TOKENS + offsets
        query_start = jnp.max(
            jnp.where(doc_ends[None, :] <= query_pos[:, None], doc_ends[None, :], 0), axis=1
        )
        unit_start = jnp.max(jnp.where(doc_ends <= position_unit * UNIT_TOKENS, doc_ends, 0))
        first_unit = unit_start // UNIT_TOKENS
        query_piece = shaped_queries[query_unit * UNIT_TOKENS : (query_unit + 1) * UNIT_TOKENS]

        def tile_at(carried, step, pair_piece):
            key_unit = position_unit - step
            key_pos = key_unit * UNIT_TOKENS + offsets
            return tile_update(
                carried,
                query_piece,
                pair_piece[:, :HEAD_SIZE],
                pair_piece[:, HEAD_SIZE:],
                query_pos,
                query_start,
                key_pos,
            )

        def visit(step, carried):
            key_row_unit = inverse[position_unit - step]
            key_row = (key_row_unit % group_units) * UNIT_TOKENS
            pair_piece = lax.dynamic_slice(
                everyone,
                (key_row_unit // group_units, key_row, 0),
                (1, UNIT_TOKENS, 2 * HEAD_SIZE),
            )[0]
            return tile_at(carried, step, pair_piece)

        running = (
            jnp.full((heads_here, UNIT_TOKENS), NEG_FILL, jnp.float32),
            jnp.zeros((heads_here, UNIT_TOKENS), jnp.float32),
            jnp.zeros((UNIT_TOKENS, heads_here, HEAD_SIZE), jnp.float32),
        )
        own_row = query_unit * UNIT_TOKENS
        running = tile_at(running, 0, own_pairs[own_row : own_row + UNIT_TOKENS])
        _, totals, accumulated = lax.fori_loop(
            1, position_unit - first_unit + 1, visit, running
        )
        outputs.append(
            (accumulated / totals.T[:, :, None])
            .reshape(UNIT_TOKENS, heads_here * HEAD_SIZE)
            .astype(jnp.bfloat16)
        )
    normalized = jnp.concatenate(outputs, axis=0) if len(outputs) > 1 else outputs[0]
    return lax.all_to_all(normalized, "inner", split_axis=0, concat_axis=1, tiled=True)


def solution(mesh):
    placed = (
        P(("outer", "inner"), None),
        P(("outer", "inner"), None),
        P(("outer", "inner"), None),
        P(),
        P(),
    )
    return jax.shard_map(
        body, mesh=mesh, in_specs=placed, out_specs=P(("outer", "inner"), None), check_vma=False
    )
```

```python
import jax
import jax.numpy as jnp
from jax import lax
from jax.sharding import PartitionSpec as P

QUERY_HEADS = 32
KEY_VALUE_HEADS = 4
HEAD_SIZE = 128
UNIT_TOKENS = 512


NEG_FILL = -1e30


def tile_update(running, query_piece, key_piece, value_piece, query_pos, query_start, key_pos):
    old_max, old_total, old_accum = running
    tile_rows, heads_here, _ = query_piece.shape
    allowed = (key_pos[None, :] >= query_start[:, None]) & (key_pos[None, :] <= query_pos[:, None])
    scores = jnp.einsum(
        "qhd,kd->hqk", query_piece, key_piece, preferred_element_type=jnp.float32
    ) * HEAD_SIZE ** (-0.5)
    scores = jnp.where(allowed[None], scores, NEG_FILL)
    new_max = jnp.maximum(old_max, jnp.max(scores, axis=2))
    weights = jnp.where(allowed[None], jnp.exp(scores - new_max[:, :, None]), 0.0)
    factor = jnp.exp(old_max - new_max)
    new_total = old_total * factor + jnp.sum(weights, axis=2)
    update = jnp.einsum(
        "hqk,kd->qhd",
        weights.astype(jnp.bfloat16),
        value_piece,
        preferred_element_type=jnp.float32,
    )
    new_accum = old_accum * factor.T[:, :, None] + update
    return (new_max, new_total, new_accum)


def body(query_rows, key_matrix, value_matrix, unit_order, doc_lengths):
    inner_steps = lax.axis_size("inner")
    token_total = query_rows.shape[0]
    group_rows = inner_steps * token_total
    heads_here = QUERY_HEADS // inner_steps
    head_copies = inner_steps // KEY_VALUE_HEADS
    query_width = heads_here * HEAD_SIZE
    query_width = heads_here * HEAD_SIZE

    def widened_heads(score_matrix):
        return jnp.repeat(
            score_matrix.reshape(token_total, KEY_VALUE_HEADS, HEAD_SIZE), head_copies, axis=1
        )

    pairs = jnp.concatenate([widened_heads(key_matrix), widened_heads(value_matrix)], axis=2)
    own_pairs = lax.all_to_all(pairs, "inner", split_axis=1, concat_axis=0, tiled=True)
    own_pairs = own_pairs.reshape(group_rows, 2 * HEAD_SIZE)
    outer_count = lax.axis_size("outer")
    outer_index = lax.axis_index("outer")
    received = [own_pairs]
    for distance in range(1, outer_count):
        route = [(i, (i + distance) % outer_count) for i in range(outer_count)]
        received.append(lax.ppermute(own_pairs, "outer", route))
    local_queries = lax.all_to_all(query_rows, "inner", split_axis=1, concat_axis=0, tiled=True)

    unit_count = unit_order.shape[0]
    inverse = jnp.zeros((unit_count,), jnp.int32).at[unit_order].set(
        jnp.arange(unit_count, dtype=jnp.int32)
    )
    doc_ends = jnp.cumsum(doc_lengths).astype(jnp.int32)
    group_units = group_rows // UNIT_TOKENS
    group_begin = outer_index * group_units
    offsets = jnp.arange(UNIT_TOKENS, dtype=jnp.int32)
    shaped_queries = local_queries.reshape(group_rows, heads_here, HEAD_SIZE)

    outputs = []
    for query_unit in range(group_units):
        position_unit = unit_order[group_begin + query_unit]
        query_pos = position_unit * UNIT_TOKENS + offsets
        query_start = jnp.max(
            jnp.where(doc_ends[None, :] <= query_pos[:, None], doc_ends[None, :], 0), axis=1
        )
        first_unit = query_start[0] // UNIT_TOKENS
        query_piece = shaped_queries[query_unit * UNIT_TOKENS : (query_unit + 1) * UNIT_TOKENS]

        def tile_at(carried, step, pair_piece):
            key_unit = position_unit - step
            key_pos = key_unit * UNIT_TOKENS + offsets
            return tile_update(
                carried,
                query_piece,
                pair_piece[:, :HEAD_SIZE],
                pair_piece[:, HEAD_SIZE:],
                query_pos,
                query_start,
                key_pos,
            )

        def visit(step, carried):
            key_row_unit = inverse[position_unit - step]
            source = (outer_index - key_row_unit // group_units) % outer_count
            key_row = (key_row_unit % group_units) * UNIT_TOKENS
            pair_piece = lax.switch(
                source,
                [
                    (lambda row, block=block: lax.dynamic_slice_in_dim(block, row, UNIT_TOKENS, 0))
                    for block in received
                ],
                key_row,
            )
            return tile_at(carried, step, pair_piece)

        running = (
            jnp.full((heads_here, UNIT_TOKENS), NEG_FILL, jnp.float32),
            jnp.zeros((heads_here, UNIT_TOKENS), jnp.float32),
            jnp.zeros((UNIT_TOKENS, heads_here, HEAD_SIZE), jnp.float32),
        )
        own_row = query_unit * UNIT_TOKENS
        running = tile_at(running, 0, own_pairs[own_row : own_row + UNIT_TOKENS])
        _, totals, accumulated = lax.fori_loop(
            1, position_unit - first_unit + 1, visit, running
        )
        outputs.append(
            (accumulated / totals.T[:, :, None])
            .reshape(UNIT_TOKENS, heads_here * HEAD_SIZE)
            .astype(jnp.bfloat16)
        )
    normalized = jnp.concatenate(outputs, axis=0) if len(outputs) > 1 else outputs[0]
    inner_index = lax.axis_index("inner")
    pieces = normalized.reshape(inner_steps, token_total, query_width)
    arrived = [lax.dynamic_index_in_dim(pieces, inner_index, 0, keepdims=False)]
    for distance in range(1, inner_steps):
        route = [(i, (i + distance) % inner_steps) for i in range(inner_steps)]
        outgoing = lax.dynamic_index_in_dim(
            pieces, (inner_index + distance) % inner_steps, 0, keepdims=False
        )
        arrived.append(lax.ppermute(outgoing, "inner", route))
    order = (inner_index - jnp.arange(inner_steps, dtype=jnp.int32)) % inner_steps
    placed = jnp.take(jnp.stack(arrived), order, axis=0)
    return jnp.transpose(placed, (1, 0, 2)).reshape(token_total, inner_steps * query_width)


def solution(mesh):
    placed = (
        P(("outer", "inner"), None),
        P(("outer", "inner"), None),
        P(("outer", "inner"), None),
        P(),
        P(),
    )
    return jax.shard_map(
        body, mesh=mesh, in_specs=placed, out_specs=P(("outer", "inner"), None), check_vma=False
    )
```

```python
import jax
import jax.numpy as jnp
from jax import lax
from jax.experimental import pallas as pl
from jax.sharding import PartitionSpec as P

QUERY_HEADS = 32
KEY_VALUE_HEADS = 4
HEAD_SIZE = 128
UNIT_TOKENS = 512


NEG_FILL = -1e30


def tile_kernel(
    query_ref, key_ref, value_ref, row_ref, start_ref, column_ref,
    max_ref, total_ref, accum_ref, max_out, total_out, accum_out,
):
    key_piece = key_ref[...]
    value_piece = value_ref[...]
    column = column_ref[...]
    allowed = (column >= start_ref[...]) & (column <= row_ref[...])
    for head in range(max_ref.shape[1]):
        lanes = slice(head * HEAD_SIZE, (head + 1) * HEAD_SIZE)
        scores = lax.dot_general(
            query_ref[:, lanes],
            key_piece,
            (((1,), (1,)), ((), ())),
            preferred_element_type=jnp.float32,
        ) * HEAD_SIZE ** (-0.5)
        scores = jnp.where(allowed, scores, NEG_FILL)
        old_max = max_ref[:, head : head + 1]
        new_max = jnp.maximum(old_max, jnp.max(scores, axis=1, keepdims=True))
        weights = jnp.where(allowed, jnp.exp(scores - new_max), 0.0)
        factor = jnp.exp(old_max - new_max)
        total_out[:, head : head + 1] = total_ref[:, head : head + 1] * factor + jnp.sum(
            weights, axis=1, keepdims=True
        )
        max_out[:, head : head + 1] = new_max
        update = jnp.dot(
            weights.astype(jnp.bfloat16), value_piece, preferred_element_type=jnp.float32
        )
        accum_out[:, lanes] = accum_ref[:, lanes] * factor + update


def tile_update(running, query_piece, key_piece, value_piece, query_pos, query_start, key_pos):
    return pl.pallas_call(
        tile_kernel,
        out_shape=tuple(jax.ShapeDtypeStruct(part.shape, part.dtype) for part in running),
        input_output_aliases={6: 0, 7: 1, 8: 2},
    )(
        query_piece,
        key_piece,
        value_piece,
        query_pos[:, None],
        query_start[:, None],
        key_pos[None, :],
        *running,
    )


def body(query_rows, key_matrix, value_matrix, unit_order, doc_lengths):
    inner_steps = lax.axis_size("inner")
    token_total = query_rows.shape[0]
    group_rows = inner_steps * token_total
    heads_here = QUERY_HEADS // inner_steps
    head_copies = inner_steps // KEY_VALUE_HEADS
    query_width = heads_here * HEAD_SIZE
    query_width = heads_here * HEAD_SIZE

    def widened_heads(score_matrix):
        return jnp.repeat(
            score_matrix.reshape(token_total, KEY_VALUE_HEADS, HEAD_SIZE), head_copies, axis=1
        )

    pairs = jnp.concatenate([widened_heads(key_matrix), widened_heads(value_matrix)], axis=2)
    own_pairs = lax.all_to_all(pairs, "inner", split_axis=1, concat_axis=0, tiled=True)
    own_pairs = own_pairs.reshape(group_rows, 2 * HEAD_SIZE)
    outer_count = lax.axis_size("outer")
    outer_index = lax.axis_index("outer")
    received = [own_pairs]
    for distance in range(1, outer_count):
        route = [(i, (i + distance) % outer_count) for i in range(outer_count)]
        received.append(lax.ppermute(own_pairs, "outer", route))
    local_queries = lax.all_to_all(query_rows, "inner", split_axis=1, concat_axis=0, tiled=True)

    unit_count = unit_order.shape[0]
    inverse = jnp.zeros((unit_count,), jnp.int32).at[unit_order].set(
        jnp.arange(unit_count, dtype=jnp.int32)
    )
    doc_ends = jnp.cumsum(doc_lengths).astype(jnp.int32)
    group_units = group_rows // UNIT_TOKENS
    group_begin = outer_index * group_units
    offsets = jnp.arange(UNIT_TOKENS, dtype=jnp.int32)

    outputs = []
    for query_unit in range(group_units):
        position_unit = unit_order[group_begin + query_unit]
        query_pos = position_unit * UNIT_TOKENS + offsets
        query_start = jnp.max(
            jnp.where(doc_ends[None, :] <= query_pos[:, None], doc_ends[None, :], 0), axis=1
        )
        first_unit = query_start[0] // UNIT_TOKENS
        query_piece = local_queries[query_unit * UNIT_TOKENS : (query_unit + 1) * UNIT_TOKENS]

        def tile_at(carried, step, pair_piece):
            key_unit = position_unit - step
            key_pos = key_unit * UNIT_TOKENS + offsets
            return tile_update(
                carried,
                query_piece,
                pair_piece[:, :HEAD_SIZE],
                pair_piece[:, HEAD_SIZE:],
                query_pos,
                query_start,
                key_pos,
            )

        def visit(step, carried):
            key_row_unit = inverse[position_unit - step]
            source = (outer_index - key_row_unit // group_units) % outer_count
            key_row = (key_row_unit % group_units) * UNIT_TOKENS
            pair_piece = lax.switch(
                source,
                [
                    (lambda row, block=block: lax.dynamic_slice_in_dim(block, row, UNIT_TOKENS, 0))
                    for block in received
                ],
                key_row,
            )
            return tile_at(carried, step, pair_piece)

        running = (
            jnp.full((UNIT_TOKENS, heads_here), NEG_FILL, jnp.float32),
            jnp.zeros((UNIT_TOKENS, heads_here), jnp.float32),
            jnp.zeros((UNIT_TOKENS, query_width), jnp.float32),
        )
        own_row = query_unit * UNIT_TOKENS
        running = tile_at(running, 0, own_pairs[own_row : own_row + UNIT_TOKENS])
        _, totals, accumulated = lax.fori_loop(
            1, position_unit - first_unit + 1, visit, running
        )
        outputs.append(
            (
                accumulated.reshape(UNIT_TOKENS, heads_here, HEAD_SIZE) / totals[:, :, None]
            )
            .reshape(UNIT_TOKENS, query_width)
            .astype(jnp.bfloat16)
        )
    normalized = jnp.concatenate(outputs, axis=0) if len(outputs) > 1 else outputs[0]
    inner_index = lax.axis_index("inner")
    pieces = normalized.reshape(inner_steps, token_total, query_width)
    arrived = [lax.dynamic_index_in_dim(pieces, inner_index, 0, keepdims=False)]
    for distance in range(1, inner_steps):
        route = [(i, (i + distance) % inner_steps) for i in range(inner_steps)]
        outgoing = lax.dynamic_index_in_dim(
            pieces, (inner_index + distance) % inner_steps, 0, keepdims=False
        )
        arrived.append(lax.ppermute(outgoing, "inner", route))
    order = (inner_index - jnp.arange(inner_steps, dtype=jnp.int32)) % inner_steps
    placed = jnp.take(jnp.stack(arrived), order, axis=0)
    return jnp.transpose(placed, (1, 0, 2)).reshape(token_total, inner_steps * query_width)


def solution(mesh):
    placed = (
        P(("outer", "inner"), None),
        P(("outer", "inner"), None),
        P(("outer", "inner"), None),
        P(),
        P(),
    )
    return jax.shard_map(
        body, mesh=mesh, in_specs=placed, out_specs=P(("outer", "inner"), None), check_vma=False
    )
```

```python
import jax
import jax.numpy as jnp
from jax import lax
from jax.experimental import pallas as pl
from jax.experimental.pallas import tpu as pltpu
from jax.sharding import PartitionSpec as P

QUERY_HEADS = 32
KEY_VALUE_HEADS = 4
HEAD_SIZE = 128
UNIT_TOKENS = 512


NEG_FILL = -1e30


ROW_BLOCK = 128


def tile_kernel(
    needed_ref, query_ref, key_ref, value_ref, row_ref, start_ref, column_ref,
    max_ref, total_ref, accum_ref, max_out, total_out, accum_out,
):
    block = pl.program_id(0)
    head = pl.program_id(1)

    @pl.when(head == 0)
    def _():
        max_out[...] = max_ref[...]
        total_out[...] = total_ref[...]

    @pl.when(needed_ref[block] > 0)
    def _():
        column = column_ref[...]
        allowed = (column >= start_ref[...]) & (column <= row_ref[...])
        scores = lax.dot_general(
            query_ref[...],
            key_ref[...],
            (((1,), (1,)), ((), ())),
            preferred_element_type=jnp.float32,
        ) * HEAD_SIZE ** (-0.5)
        scores = jnp.where(allowed, scores, NEG_FILL)
        heads = max_out.shape[1]
        picked = lax.broadcasted_iota(jnp.int32, (1, heads), 1) == head
        old_maxes = max_out[...]
        old_max = jnp.sum(jnp.where(picked, old_maxes, 0.0), axis=1, keepdims=True)
        new_max = jnp.maximum(old_max, jnp.max(scores, axis=1, keepdims=True))
        weights = jnp.where(allowed, jnp.exp(scores - new_max), 0.0)
        factor = jnp.exp(old_max - new_max)
        old_totals = total_out[...]
        old_total = jnp.sum(jnp.where(picked, old_totals, 0.0), axis=1, keepdims=True)
        new_total = old_total * factor + jnp.sum(weights, axis=1, keepdims=True)
        max_out[...] = jnp.where(picked, new_max, old_maxes)
        total_out[...] = jnp.where(picked, new_total, old_totals)
        update = jnp.dot(
            weights.astype(jnp.bfloat16), value_ref[...], preferred_element_type=jnp.float32
        )
        accum_out[...] = accum_ref[...] * factor + update

    @pl.when(needed_ref[block] == 0)
    def _():
        accum_out[...] = accum_ref[...]


def tile_update(running, query_piece, key_piece, value_piece, query_pos, query_start, key_pos):
    rows, heads = running[0].shape
    blocks = rows // ROW_BLOCK
    block_rows = lambda b, h, needed: (b, 0)
    block_heads = lambda b, h, needed: (b, h)
    whole = lambda b, h, needed: (0, 0)
    key_last = key_pos[-1]
    block_start = query_start.reshape(blocks, ROW_BLOCK)[:, 0]
    block_end = query_pos.reshape(blocks, ROW_BLOCK)[:, -1]
    needed = ((block_start <= key_last) & (key_pos[0] <= block_end)).astype(jnp.int32)
    spec = pltpu.PrefetchScalarGridSpec(
        num_scalar_prefetch=1,
        grid=(blocks, heads),
        in_specs=[
            pl.BlockSpec((ROW_BLOCK, HEAD_SIZE), block_heads),
            pl.BlockSpec((key_piece.shape[0], HEAD_SIZE), whole),
            pl.BlockSpec((key_piece.shape[0], HEAD_SIZE), whole),
            pl.BlockSpec((ROW_BLOCK, 1), block_rows),
            pl.BlockSpec((ROW_BLOCK, 1), block_rows),
            pl.BlockSpec((1, key_piece.shape[0]), whole),
            pl.BlockSpec((ROW_BLOCK, heads), block_rows),
            pl.BlockSpec((ROW_BLOCK, heads), block_rows),
            pl.BlockSpec((ROW_BLOCK, HEAD_SIZE), block_heads),
        ],
        out_specs=[
            pl.BlockSpec((ROW_BLOCK, heads), block_rows),
            pl.BlockSpec((ROW_BLOCK, heads), block_rows),
            pl.BlockSpec((ROW_BLOCK, HEAD_SIZE), block_heads),
        ],
    )
    return tuple(
        pl.pallas_call(
            tile_kernel,
            grid_spec=spec,
            out_shape=[jax.ShapeDtypeStruct(part.shape, part.dtype) for part in running],
            input_output_aliases={7: 0, 8: 1, 9: 2},
        )(
            needed,
            query_piece,
            key_piece,
            value_piece,
            query_pos[:, None],
            query_start[:, None],
            key_pos[None, :],
            *running,
        )
    )


def body(query_rows, key_matrix, value_matrix, unit_order, doc_lengths):
    inner_steps = lax.axis_size("inner")
    token_total = query_rows.shape[0]
    group_rows = inner_steps * token_total
    heads_here = QUERY_HEADS // inner_steps
    head_copies = inner_steps // KEY_VALUE_HEADS
    query_width = heads_here * HEAD_SIZE
    query_width = heads_here * HEAD_SIZE

    def widened_heads(score_matrix):
        return jnp.repeat(
            score_matrix.reshape(token_total, KEY_VALUE_HEADS, HEAD_SIZE), head_copies, axis=1
        )

    pairs = jnp.concatenate([widened_heads(key_matrix), widened_heads(value_matrix)], axis=2)
    own_pairs = lax.all_to_all(pairs, "inner", split_axis=1, concat_axis=0, tiled=True)
    own_pairs = own_pairs.reshape(group_rows, 2 * HEAD_SIZE)
    outer_count = lax.axis_size("outer")
    outer_index = lax.axis_index("outer")
    received = [own_pairs]
    for distance in range(1, outer_count):
        route = [(i, (i + distance) % outer_count) for i in range(outer_count)]
        received.append(lax.ppermute(own_pairs, "outer", route))
    local_queries = lax.all_to_all(query_rows, "inner", split_axis=1, concat_axis=0, tiled=True)

    unit_count = unit_order.shape[0]
    inverse = jnp.zeros((unit_count,), jnp.int32).at[unit_order].set(
        jnp.arange(unit_count, dtype=jnp.int32)
    )
    doc_ends = jnp.cumsum(doc_lengths).astype(jnp.int32)
    group_units = group_rows // UNIT_TOKENS
    group_begin = outer_index * group_units
    offsets = jnp.arange(UNIT_TOKENS, dtype=jnp.int32)

    outputs = []
    for query_unit in range(group_units):
        position_unit = unit_order[group_begin + query_unit]
        query_pos = position_unit * UNIT_TOKENS + offsets
        query_start = jnp.max(
            jnp.where(doc_ends[None, :] <= query_pos[:, None], doc_ends[None, :], 0), axis=1
        )
        first_unit = query_start[0] // UNIT_TOKENS
        query_piece = local_queries[query_unit * UNIT_TOKENS : (query_unit + 1) * UNIT_TOKENS]

        def tile_at(carried, step, pair_piece):
            key_unit = position_unit - step
            key_pos = key_unit * UNIT_TOKENS + offsets
            return tile_update(
                carried,
                query_piece,
                pair_piece[:, :HEAD_SIZE],
                pair_piece[:, HEAD_SIZE:],
                query_pos,
                query_start,
                key_pos,
            )

        def visit(step, carried):
            key_row_unit = inverse[position_unit - step]
            source = (outer_index - key_row_unit // group_units) % outer_count
            key_row = (key_row_unit % group_units) * UNIT_TOKENS
            pair_piece = lax.switch(
                source,
                [
                    (lambda row, block=block: lax.dynamic_slice_in_dim(block, row, UNIT_TOKENS, 0))
                    for block in received
                ],
                key_row,
            )
            return tile_at(carried, step, pair_piece)

        running = (
            jnp.full((UNIT_TOKENS, heads_here), NEG_FILL, jnp.float32),
            jnp.zeros((UNIT_TOKENS, heads_here), jnp.float32),
            jnp.zeros((UNIT_TOKENS, query_width), jnp.float32),
        )
        own_row = query_unit * UNIT_TOKENS
        running = tile_at(running, 0, own_pairs[own_row : own_row + UNIT_TOKENS])
        _, totals, accumulated = lax.fori_loop(
            1, position_unit - first_unit + 1, visit, running
        )
        outputs.append(
            (
                accumulated.reshape(UNIT_TOKENS, heads_here, HEAD_SIZE) / totals[:, :, None]
            )
            .reshape(UNIT_TOKENS, query_width)
            .astype(jnp.bfloat16)
        )
    normalized = jnp.concatenate(outputs, axis=0) if len(outputs) > 1 else outputs[0]
    inner_index = lax.axis_index("inner")
    pieces = normalized.reshape(inner_steps, token_total, query_width)
    arrived = [lax.dynamic_index_in_dim(pieces, inner_index, 0, keepdims=False)]
    for distance in range(1, inner_steps):
        route = [(i, (i + distance) % inner_steps) for i in range(inner_steps)]
        outgoing = lax.dynamic_index_in_dim(
            pieces, (inner_index + distance) % inner_steps, 0, keepdims=False
        )
        arrived.append(lax.ppermute(outgoing, "inner", route))
    order = (inner_index - jnp.arange(inner_steps, dtype=jnp.int32)) % inner_steps
    placed = jnp.take(jnp.stack(arrived), order, axis=0)
    return jnp.transpose(placed, (1, 0, 2)).reshape(token_total, inner_steps * query_width)


def solution(mesh):
    placed = (
        P(("outer", "inner"), None),
        P(("outer", "inner"), None),
        P(("outer", "inner"), None),
        P(),
        P(),
    )
    return jax.shard_map(
        body, mesh=mesh, in_specs=placed, out_specs=P(("outer", "inner"), None), check_vma=False
    )
```

```python
import jax
import jax.numpy as jnp
from jax import lax
from jax.sharding import PartitionSpec as P

QUERY_HEADS = 32
KEY_VALUE_HEADS = 4
HEAD_SIZE = 128
UNIT_TOKENS = 512


NEG_FILL = -1e30


def tile_update(running, query_piece, key_piece, value_piece, query_pos, query_start, key_pos):
    old_max, old_total, old_accum = running
    tile_rows, heads_here, _ = query_piece.shape
    allowed = (key_pos[None, :] >= query_start[:, None]) & (key_pos[None, :] <= query_pos[:, None])
    scores = jnp.einsum(
        "qhd,kd->hqk", query_piece, key_piece, preferred_element_type=jnp.float32
    ) * HEAD_SIZE ** (-0.5)
    scores = jnp.where(allowed[None], scores, NEG_FILL)
    new_max = jnp.maximum(old_max, jnp.max(scores, axis=2))
    weights = jnp.where(allowed[None], jnp.exp(scores - new_max[:, :, None]), 0.0)
    factor = jnp.exp(old_max - new_max)
    new_total = old_total * factor + jnp.sum(weights, axis=2)
    update = jnp.einsum(
        "hqk,kd->qhd",
        weights.astype(jnp.bfloat16),
        value_piece,
        preferred_element_type=jnp.float32,
    )
    new_accum = old_accum * factor.T[:, :, None] + update
    return (new_max, new_total, new_accum)


def body(query_rows, key_matrix, value_matrix, unit_order, doc_lengths):
    inner_steps = lax.axis_size("inner")
    token_total = query_rows.shape[0]
    group_rows = inner_steps * token_total
    heads_here = QUERY_HEADS // inner_steps
    head_copies = inner_steps // KEY_VALUE_HEADS
    query_width = heads_here * HEAD_SIZE
    query_width = heads_here * HEAD_SIZE

    def widened_heads(score_matrix):
        return jnp.repeat(
            score_matrix.reshape(token_total, KEY_VALUE_HEADS, HEAD_SIZE), head_copies, axis=1
        )

    pairs = jnp.concatenate([widened_heads(key_matrix), widened_heads(value_matrix)], axis=2)
    own_pairs = lax.all_to_all(pairs, "inner", split_axis=1, concat_axis=0, tiled=True)
    own_pairs = own_pairs.reshape(group_rows, 2 * HEAD_SIZE)
    outer_count = lax.axis_size("outer")
    outer_index = lax.axis_index("outer")
    unit_count = unit_order.shape[0]
    inverse = jnp.zeros((unit_count,), jnp.int32).at[unit_order].set(
        jnp.arange(unit_count, dtype=jnp.int32)
    )
    doc_ends = jnp.cumsum(doc_lengths).astype(jnp.int32)
    group_units = group_rows // UNIT_TOKENS
    group_begin = outer_index * group_units
    offsets = jnp.arange(UNIT_TOKENS, dtype=jnp.int32)
    unit_facts = []
    for query_unit in range(group_units):
        position_unit = unit_order[group_begin + query_unit]
        query_pos = position_unit * UNIT_TOKENS + offsets
        query_start = jnp.max(
            jnp.where(doc_ends[None, :] <= query_pos[:, None], doc_ends[None, :], 0), axis=1
        )
        first_unit = query_start[0] // UNIT_TOKENS
        unit_facts.append((position_unit, query_pos, query_start, first_unit))
    own_pairs, inverse, unit_facts, query_rows = lax.optimization_barrier(
        (own_pairs, inverse, unit_facts, query_rows)
    )
    received = [own_pairs]
    for distance in range(1, outer_count):
        route = [(i, (i + distance) % outer_count) for i in range(outer_count)]
        received.append(lax.ppermute(own_pairs, "outer", route))
    local_queries = lax.all_to_all(query_rows, "inner", split_axis=1, concat_axis=0, tiled=True)
    shaped_queries = local_queries.reshape(group_rows, heads_here, HEAD_SIZE)

    outputs = []
    for query_unit in range(group_units):
        position_unit, query_pos, query_start, first_unit = unit_facts[query_unit]
        query_piece = shaped_queries[query_unit * UNIT_TOKENS : (query_unit + 1) * UNIT_TOKENS]

        def tile_at(carried, step, pair_piece):
            key_unit = position_unit - step
            key_pos = key_unit * UNIT_TOKENS + offsets
            return tile_update(
                carried,
                query_piece,
                pair_piece[:, :HEAD_SIZE],
                pair_piece[:, HEAD_SIZE:],
                query_pos,
                query_start,
                key_pos,
            )

        def visit(step, carried):
            key_row_unit = inverse[position_unit - step]
            source = (outer_index - key_row_unit // group_units) % outer_count
            key_row = (key_row_unit % group_units) * UNIT_TOKENS
            pair_piece = lax.switch(
                source,
                [
                    (lambda row, block=block: lax.dynamic_slice_in_dim(block, row, UNIT_TOKENS, 0))
                    for block in received
                ],
                key_row,
            )
            return tile_at(carried, step, pair_piece)

        running = (
            jnp.full((heads_here, UNIT_TOKENS), NEG_FILL, jnp.float32),
            jnp.zeros((heads_here, UNIT_TOKENS), jnp.float32),
            jnp.zeros((UNIT_TOKENS, heads_here, HEAD_SIZE), jnp.float32),
        )
        own_row = query_unit * UNIT_TOKENS
        running = tile_at(running, 0, own_pairs[own_row : own_row + UNIT_TOKENS])
        _, totals, accumulated = lax.fori_loop(
            1, position_unit - first_unit + 1, visit, running
        )
        outputs.append(
            (accumulated / totals.T[:, :, None])
            .reshape(UNIT_TOKENS, heads_here * HEAD_SIZE)
            .astype(jnp.bfloat16)
        )
    normalized = jnp.concatenate(outputs, axis=0) if len(outputs) > 1 else outputs[0]
    inner_index = lax.axis_index("inner")
    pieces = normalized.reshape(inner_steps, token_total, query_width)
    arrived = [lax.dynamic_index_in_dim(pieces, inner_index, 0, keepdims=False)]
    for distance in range(1, inner_steps):
        route = [(i, (i + distance) % inner_steps) for i in range(inner_steps)]
        outgoing = lax.dynamic_index_in_dim(
            pieces, (inner_index + distance) % inner_steps, 0, keepdims=False
        )
        arrived.append(lax.ppermute(outgoing, "inner", route))
    order = (inner_index - jnp.arange(inner_steps, dtype=jnp.int32)) % inner_steps
    placed = jnp.take(jnp.stack(arrived), order, axis=0)
    return jnp.transpose(placed, (1, 0, 2)).reshape(token_total, inner_steps * query_width)


def solution(mesh):
    placed = (
        P(("outer", "inner"), None),
        P(("outer", "inner"), None),
        P(("outer", "inner"), None),
        P(),
        P(),
    )
    return jax.shard_map(
        body, mesh=mesh, in_specs=placed, out_specs=P(("outer", "inner"), None), check_vma=False
    )
```

```python
import jax
import jax.numpy as jnp
from jax import lax
from jax.sharding import PartitionSpec as P

QUERY_HEADS = 32
KEY_VALUE_HEADS = 4
HEAD_SIZE = 128
UNIT_TOKENS = 512


NEG_FILL = -1e30


def tile_update(running, query_piece, key_piece, value_piece, query_pos, query_start, key_pos):
    old_max, old_total, old_accum = running
    tile_rows, heads_here, _ = query_piece.shape
    allowed = (key_pos[None, :] >= query_start[:, None]) & (key_pos[None, :] <= query_pos[:, None])
    scores = jnp.einsum(
        "qhd,kd->hqk", query_piece, key_piece, preferred_element_type=jnp.float32
    ) * HEAD_SIZE ** (-0.5)
    scores = jnp.where(allowed[None], scores, NEG_FILL)
    new_max = jnp.maximum(old_max, jnp.max(scores, axis=2))
    weights = jnp.where(allowed[None], jnp.exp(scores - new_max[:, :, None]), 0.0)
    factor = jnp.exp(old_max - new_max)
    new_total = old_total * factor + jnp.sum(weights, axis=2)
    update = jnp.einsum(
        "hqk,kd->qhd",
        weights.astype(jnp.bfloat16),
        value_piece,
        preferred_element_type=jnp.float32,
    )
    new_accum = old_accum * factor.T[:, :, None] + update
    return (new_max, new_total, new_accum)


def swap_inner(pieces, inner_index, inner_steps):
    arrived = [lax.dynamic_index_in_dim(pieces, inner_index, 0, keepdims=False)]
    for distance in range(1, inner_steps):
        route = [(i, (i + distance) % inner_steps) for i in range(inner_steps)]
        outgoing = lax.dynamic_index_in_dim(
            pieces, (inner_index + distance) % inner_steps, 0, keepdims=False
        )
        arrived.append(lax.ppermute(outgoing, "inner", route))
    order = (inner_index - jnp.arange(inner_steps, dtype=jnp.int32)) % inner_steps
    return jnp.take(jnp.stack(arrived), order, axis=0)


def body(query_rows, key_matrix, value_matrix, unit_order, doc_lengths):
    inner_steps = lax.axis_size("inner")
    token_total = query_rows.shape[0]
    group_rows = inner_steps * token_total
    heads_here = QUERY_HEADS // inner_steps
    head_copies = inner_steps // KEY_VALUE_HEADS
    query_width = heads_here * HEAD_SIZE
    query_width = heads_here * HEAD_SIZE

    def widened_heads(score_matrix):
        return jnp.repeat(
            score_matrix.reshape(token_total, KEY_VALUE_HEADS, HEAD_SIZE), head_copies, axis=1
        )

    pairs = jnp.concatenate([widened_heads(key_matrix), widened_heads(value_matrix)], axis=2)
    inner_index = lax.axis_index("inner")
    own_pairs = swap_inner(jnp.transpose(pairs, (1, 0, 2)), inner_index, inner_steps)
    own_pairs = own_pairs.reshape(group_rows, 2 * HEAD_SIZE)
    outer_count = lax.axis_size("outer")
    outer_index = lax.axis_index("outer")
    unit_count = unit_order.shape[0]
    inverse = jnp.zeros((unit_count,), jnp.int32).at[unit_order].set(
        jnp.arange(unit_count, dtype=jnp.int32)
    )
    doc_ends = jnp.cumsum(doc_lengths).astype(jnp.int32)
    group_units = group_rows // UNIT_TOKENS
    group_begin = outer_index * group_units
    offsets = jnp.arange(UNIT_TOKENS, dtype=jnp.int32)
    unit_facts = []
    for query_unit in range(group_units):
        position_unit = unit_order[group_begin + query_unit]
        query_pos = position_unit * UNIT_TOKENS + offsets
        query_start = jnp.max(
            jnp.where(doc_ends[None, :] <= query_pos[:, None], doc_ends[None, :], 0), axis=1
        )
        first_unit = query_start[0] // UNIT_TOKENS
        unit_facts.append((position_unit, query_pos, query_start, first_unit))
    own_pairs, inverse, unit_facts, query_rows = lax.optimization_barrier(
        (own_pairs, inverse, unit_facts, query_rows)
    )
    received = [own_pairs]
    for distance in range(1, outer_count):
        route = [(i, (i + distance) % outer_count) for i in range(outer_count)]
        received.append(lax.ppermute(own_pairs, "outer", route))
    local_queries = lax.all_to_all(query_rows, "inner", split_axis=1, concat_axis=0, tiled=True)
    shaped_queries = local_queries.reshape(group_rows, heads_here, HEAD_SIZE)

    outputs = []
    for query_unit in range(group_units):
        position_unit, query_pos, query_start, first_unit = unit_facts[query_unit]
        query_piece = shaped_queries[query_unit * UNIT_TOKENS : (query_unit + 1) * UNIT_TOKENS]

        def tile_at(carried, step, pair_piece):
            key_unit = position_unit - step
            key_pos = key_unit * UNIT_TOKENS + offsets
            return tile_update(
                carried,
                query_piece,
                pair_piece[:, :HEAD_SIZE],
                pair_piece[:, HEAD_SIZE:],
                query_pos,
                query_start,
                key_pos,
            )

        def visit(step, carried):
            key_row_unit = inverse[position_unit - step]
            source = (outer_index - key_row_unit // group_units) % outer_count
            key_row = (key_row_unit % group_units) * UNIT_TOKENS
            pair_piece = lax.switch(
                source,
                [
                    (lambda row, block=block: lax.dynamic_slice_in_dim(block, row, UNIT_TOKENS, 0))
                    for block in received
                ],
                key_row,
            )
            return tile_at(carried, step, pair_piece)

        running = (
            jnp.full((heads_here, UNIT_TOKENS), NEG_FILL, jnp.float32),
            jnp.zeros((heads_here, UNIT_TOKENS), jnp.float32),
            jnp.zeros((UNIT_TOKENS, heads_here, HEAD_SIZE), jnp.float32),
        )
        own_row = query_unit * UNIT_TOKENS
        running = tile_at(running, 0, own_pairs[own_row : own_row + UNIT_TOKENS])
        _, totals, accumulated = lax.fori_loop(
            1, position_unit - first_unit + 1, visit, running
        )
        outputs.append(
            (accumulated / totals.T[:, :, None])
            .reshape(UNIT_TOKENS, heads_here * HEAD_SIZE)
            .astype(jnp.bfloat16)
        )
    normalized = jnp.concatenate(outputs, axis=0) if len(outputs) > 1 else outputs[0]
    pieces = normalized.reshape(inner_steps, token_total, query_width)
    placed = swap_inner(pieces, inner_index, inner_steps)
    return jnp.transpose(placed, (1, 0, 2)).reshape(token_total, inner_steps * query_width)


def solution(mesh):
    placed = (
        P(("outer", "inner"), None),
        P(("outer", "inner"), None),
        P(("outer", "inner"), None),
        P(),
        P(),
    )
    return jax.shard_map(
        body, mesh=mesh, in_specs=placed, out_specs=P(("outer", "inner"), None), check_vma=False
    )
```

```python
import jax
import jax.numpy as jnp
from jax import lax
from jax.sharding import PartitionSpec as P

QUERY_HEADS = 32
KEY_VALUE_HEADS = 4
HEAD_SIZE = 128
UNIT_TOKENS = 512


NEG_FILL = -1e30


def tile_update(running, query_piece, key_piece, value_piece, query_pos, query_start, key_pos):
    old_max, old_total, old_accum = running
    tile_rows, heads_here, _ = query_piece.shape
    allowed = (key_pos[None, :] >= query_start[:, None]) & (key_pos[None, :] <= query_pos[:, None])
    scores = jnp.einsum(
        "qhd,kd->hqk", query_piece, key_piece, preferred_element_type=jnp.float32
    ) * HEAD_SIZE ** (-0.5)
    scores = jnp.where(allowed[None], scores, NEG_FILL)
    new_max = jnp.maximum(old_max, jnp.max(scores, axis=2))
    weights = jnp.where(allowed[None], jnp.exp(scores - new_max[:, :, None]), 0.0)
    factor = jnp.exp(old_max - new_max)
    new_total = old_total * factor + jnp.sum(weights, axis=2)
    update = jnp.einsum(
        "hqk,kd->qhd",
        weights.astype(jnp.bfloat16),
        value_piece,
        preferred_element_type=jnp.float32,
    )
    new_accum = old_accum * factor.T[:, :, None] + update
    return (new_max, new_total, new_accum)


def swap_inner(pieces, inner_index, inner_steps):
    arrived = [lax.dynamic_index_in_dim(pieces, inner_index, 0, keepdims=False)]
    for distance in range(1, inner_steps):
        route = [(i, (i + distance) % inner_steps) for i in range(inner_steps)]
        outgoing = lax.dynamic_index_in_dim(
            pieces, (inner_index + distance) % inner_steps, 0, keepdims=False
        )
        arrived.append(lax.ppermute(outgoing, "inner", route))
    order = (inner_index - jnp.arange(inner_steps, dtype=jnp.int32)) % inner_steps
    return jnp.take(jnp.stack(arrived), order, axis=0)


def body(query_rows, key_matrix, value_matrix, unit_order, doc_lengths):
    inner_steps = lax.axis_size("inner")
    token_total = query_rows.shape[0]
    group_rows = inner_steps * token_total
    heads_here = QUERY_HEADS // inner_steps
    head_copies = inner_steps // KEY_VALUE_HEADS
    query_width = heads_here * HEAD_SIZE
    query_width = heads_here * HEAD_SIZE

    def widened_heads(score_matrix):
        return jnp.repeat(
            score_matrix.reshape(token_total, KEY_VALUE_HEADS, HEAD_SIZE), head_copies, axis=1
        )

    pairs = jnp.concatenate([widened_heads(key_matrix), widened_heads(value_matrix)], axis=2)
    inner_index = lax.axis_index("inner")
    own_pairs = swap_inner(jnp.transpose(pairs, (1, 0, 2)), inner_index, inner_steps)
    own_pairs = own_pairs.reshape(group_rows, 2 * HEAD_SIZE)
    outer_count = lax.axis_size("outer")
    outer_index = lax.axis_index("outer")
    received = [own_pairs]
    for distance in range(1, outer_count):
        route = [(i, (i + distance) % outer_count) for i in range(outer_count)]
        received.append(lax.ppermute(own_pairs, "outer", route))
    local_queries = lax.all_to_all(query_rows, "inner", split_axis=1, concat_axis=0, tiled=True)
    local_queries, early_order, early_lengths = lax.optimization_barrier(
        (local_queries, unit_order, doc_lengths)
    )
    shaped_queries = local_queries.reshape(group_rows, heads_here, HEAD_SIZE)
    unit_count = unit_order.shape[0]
    group_units = group_rows // UNIT_TOKENS
    group_begin = outer_index * group_units
    offsets = jnp.arange(UNIT_TOKENS, dtype=jnp.int32)
    early_ends = jnp.cumsum(early_lengths).astype(jnp.int32)

    outputs = []
    for query_unit in range(group_units):
        position_unit = early_order[group_begin + query_unit]
        query_pos = position_unit * UNIT_TOKENS + offsets
        query_start = jnp.max(
            jnp.where(early_ends[None, :] <= query_pos[:, None], early_ends[None, :], 0), axis=1
        )
        query_piece = shaped_queries[query_unit * UNIT_TOKENS : (query_unit + 1) * UNIT_TOKENS]

        def tile_at(carried, step, pair_piece):
            key_unit = position_unit - step
            key_pos = key_unit * UNIT_TOKENS + offsets
            return tile_update(
                carried,
                query_piece,
                pair_piece[:, :HEAD_SIZE],
                pair_piece[:, HEAD_SIZE:],
                query_pos,
                query_start,
                key_pos,
            )

        def visit(step, carried):
            key_row_unit = inverse[position_unit - step]
            source = (outer_index - key_row_unit // group_units) % outer_count
            key_row = (key_row_unit % group_units) * UNIT_TOKENS
            pair_piece = lax.switch(
                source,
                [
                    (lambda row, block=block: lax.dynamic_slice_in_dim(block, row, UNIT_TOKENS, 0))
                    for block in received
                ],
                key_row,
            )
            return tile_at(carried, step, pair_piece)

        running = (
            jnp.full((heads_here, UNIT_TOKENS), NEG_FILL, jnp.float32),
            jnp.zeros((heads_here, UNIT_TOKENS), jnp.float32),
            jnp.zeros((UNIT_TOKENS, heads_here, HEAD_SIZE), jnp.float32),
        )
        own_row = query_unit * UNIT_TOKENS
        running = tile_at(running, 0, own_pairs[own_row : own_row + UNIT_TOKENS])
        running, late_order, late_lengths = lax.optimization_barrier(
            (running, unit_order, doc_lengths)
        )
        inverse = jnp.zeros((unit_count,), jnp.int32).at[late_order].set(
            jnp.arange(unit_count, dtype=jnp.int32)
        )
        late_ends = jnp.cumsum(late_lengths).astype(jnp.int32)
        unit_start = jnp.max(
            jnp.where(late_ends <= late_order[group_begin + query_unit] * UNIT_TOKENS, late_ends, 0)
        )
        first_unit = unit_start // UNIT_TOKENS
        _, totals, accumulated = lax.fori_loop(
            1, position_unit - first_unit + 1, visit, running
        )
        outputs.append(
            (accumulated / totals.T[:, :, None])
            .reshape(UNIT_TOKENS, heads_here * HEAD_SIZE)
            .astype(jnp.bfloat16)
        )
    normalized = jnp.concatenate(outputs, axis=0) if len(outputs) > 1 else outputs[0]
    pieces = normalized.reshape(inner_steps, token_total, query_width)
    placed = swap_inner(pieces, inner_index, inner_steps)
    return jnp.transpose(placed, (1, 0, 2)).reshape(token_total, inner_steps * query_width)


def solution(mesh):
    placed = (
        P(("outer", "inner"), None),
        P(("outer", "inner"), None),
        P(("outer", "inner"), None),
        P(),
        P(),
    )
    return jax.shard_map(
        body, mesh=mesh, in_specs=placed, out_specs=P(("outer", "inner"), None), check_vma=False
    )
```

```python
import jax
import jax.numpy as jnp
from jax import lax
from jax.sharding import PartitionSpec as P

QUERY_HEADS = 32
KEY_VALUE_HEADS = 4
HEAD_SIZE = 128
UNIT_TOKENS = 512


NEG_FILL = -1e30


def tile_update(running, query_piece, key_piece, value_piece, query_pos, query_start, key_pos):
    old_max, old_total, old_accum = running
    tile_rows, heads_here, _ = query_piece.shape
    allowed = (key_pos[None, :] >= query_start[:, None]) & (key_pos[None, :] <= query_pos[:, None])
    scores = jnp.einsum(
        "qhd,kd->hqk", query_piece, key_piece, preferred_element_type=jnp.float32
    ) * HEAD_SIZE ** (-0.5)
    scores = jnp.where(allowed[None], scores, NEG_FILL)
    new_max = jnp.maximum(old_max, jnp.max(scores, axis=2))
    weights = jnp.where(allowed[None], jnp.exp(scores - new_max[:, :, None]), 0.0)
    factor = jnp.exp(old_max - new_max)
    new_total = old_total * factor + jnp.sum(weights, axis=2)
    update = jnp.einsum(
        "hqk,kd->qhd",
        weights.astype(jnp.bfloat16),
        value_piece,
        preferred_element_type=jnp.float32,
    )
    new_accum = old_accum * factor.T[:, :, None] + update
    return (new_max, new_total, new_accum)


def swap_inner(piece_at, inner_index, inner_steps):
    arrived = [piece_at(inner_index)]
    for distance in range(1, inner_steps):
        route = [(i, (i + distance) % inner_steps) for i in range(inner_steps)]
        arrived.append(lax.ppermute(piece_at((inner_index + distance) % inner_steps), "inner", route))
    order = (inner_index - jnp.arange(inner_steps, dtype=jnp.int32)) % inner_steps
    return jnp.take(jnp.stack(arrived), order, axis=0)


def body(query_rows, key_matrix, value_matrix, unit_order, doc_lengths):
    inner_steps = lax.axis_size("inner")
    token_total = query_rows.shape[0]
    group_rows = inner_steps * token_total
    heads_here = QUERY_HEADS // inner_steps
    head_copies = inner_steps // KEY_VALUE_HEADS
    query_width = heads_here * HEAD_SIZE
    query_width = heads_here * HEAD_SIZE

    def widened_heads(score_matrix):
        return jnp.repeat(
            score_matrix.reshape(token_total, KEY_VALUE_HEADS, HEAD_SIZE), head_copies, axis=1
        )

    pairs = jnp.concatenate([widened_heads(key_matrix), widened_heads(value_matrix)], axis=2)
    inner_index = lax.axis_index("inner")
    pair_pieces = jnp.transpose(pairs, (1, 0, 2))
    own_pairs = swap_inner(
        lambda chunk: lax.dynamic_index_in_dim(pair_pieces, chunk, 0, keepdims=False),
        inner_index,
        inner_steps,
    )
    own_pairs = own_pairs.reshape(group_rows, 2 * HEAD_SIZE)
    outer_count = lax.axis_size("outer")
    outer_index = lax.axis_index("outer")
    received = [own_pairs]
    for distance in range(1, outer_count):
        route = [(i, (i + distance) % outer_count) for i in range(outer_count)]
        received.append(lax.ppermute(own_pairs, "outer", route))
    local_queries = lax.all_to_all(query_rows, "inner", split_axis=1, concat_axis=0, tiled=True)
    local_queries, early_order, early_lengths = lax.optimization_barrier(
        (local_queries, unit_order, doc_lengths)
    )
    shaped_queries = local_queries.reshape(group_rows, heads_here, HEAD_SIZE)
    unit_count = unit_order.shape[0]
    group_units = group_rows // UNIT_TOKENS
    group_begin = outer_index * group_units
    offsets = jnp.arange(UNIT_TOKENS, dtype=jnp.int32)
    early_ends = jnp.cumsum(early_lengths).astype(jnp.int32)

    outputs = []
    for query_unit in range(group_units):
        position_unit = early_order[group_begin + query_unit]
        query_pos = position_unit * UNIT_TOKENS + offsets
        query_start = jnp.max(
            jnp.where(early_ends[None, :] <= query_pos[:, None], early_ends[None, :], 0), axis=1
        )
        query_piece = shaped_queries[query_unit * UNIT_TOKENS : (query_unit + 1) * UNIT_TOKENS]

        def tile_at(carried, step, pair_piece):
            key_unit = position_unit - step
            key_pos = key_unit * UNIT_TOKENS + offsets
            return tile_update(
                carried,
                query_piece,
                pair_piece[:, :HEAD_SIZE],
                pair_piece[:, HEAD_SIZE:],
                query_pos,
                query_start,
                key_pos,
            )

        def visit(step, carried):
            key_row_unit = inverse[position_unit - step]
            source = (outer_index - key_row_unit // group_units) % outer_count
            key_row = (key_row_unit % group_units) * UNIT_TOKENS
            pair_piece = lax.switch(
                source,
                [
                    (lambda row, block=block: lax.dynamic_slice_in_dim(block, row, UNIT_TOKENS, 0))
                    for block in received
                ],
                key_row,
            )
            return tile_at(carried, step, pair_piece)

        running = (
            jnp.full((heads_here, UNIT_TOKENS), NEG_FILL, jnp.float32),
            jnp.zeros((heads_here, UNIT_TOKENS), jnp.float32),
            jnp.zeros((UNIT_TOKENS, heads_here, HEAD_SIZE), jnp.float32),
        )
        own_row = query_unit * UNIT_TOKENS
        running = tile_at(running, 0, own_pairs[own_row : own_row + UNIT_TOKENS])
        running, late_order, late_lengths = lax.optimization_barrier(
            (running, unit_order, doc_lengths)
        )
        inverse = jnp.zeros((unit_count,), jnp.int32).at[late_order].set(
            jnp.arange(unit_count, dtype=jnp.int32)
        )
        late_ends = jnp.cumsum(late_lengths).astype(jnp.int32)
        unit_start = jnp.max(
            jnp.where(late_ends <= late_order[group_begin + query_unit] * UNIT_TOKENS, late_ends, 0)
        )
        first_unit = unit_start // UNIT_TOKENS
        _, totals, accumulated = lax.fori_loop(
            1, position_unit - first_unit + 1, visit, running
        )
        outputs.append((accumulated, totals.T))
    accumulated = jnp.concatenate([part[0] for part in outputs], axis=0)
    totals = jnp.concatenate([part[1] for part in outputs], axis=0)

    def finished(chunk):
        begin = chunk * token_total
        rows = lax.dynamic_slice_in_dim(accumulated, begin, token_total, 0)
        sums = lax.dynamic_slice_in_dim(totals, begin, token_total, 0)
        return (rows / sums[:, :, None]).reshape(token_total, query_width).astype(jnp.bfloat16)

    placed = swap_inner(finished, inner_index, inner_steps)
    return jnp.transpose(placed, (1, 0, 2)).reshape(token_total, inner_steps * query_width)


def solution(mesh):
    placed = (
        P(("outer", "inner"), None),
        P(("outer", "inner"), None),
        P(("outer", "inner"), None),
        P(),
        P(),
    )
    return jax.shard_map(
        body, mesh=mesh, in_specs=placed, out_specs=P(("outer", "inner"), None), check_vma=False
    )
```

```python
import jax
import jax.numpy as jnp
from jax import lax
from jax.sharding import PartitionSpec as P

QUERY_HEADS = 32
KEY_VALUE_HEADS = 4
HEAD_SIZE = 128
UNIT_TOKENS = 512


NEG_FILL = -1e30


def tile_update(running, query_piece, key_piece, value_piece, query_pos, query_start, key_pos):
    old_max, old_total, old_accum = running
    tile_rows, heads_here, _ = query_piece.shape
    allowed = (key_pos[None, :] >= query_start[:, None]) & (key_pos[None, :] <= query_pos[:, None])
    scores = jnp.einsum(
        "qhd,kd->hqk", query_piece, key_piece, preferred_element_type=jnp.float32
    ) * HEAD_SIZE ** (-0.5)
    scores = jnp.where(allowed[None], scores, NEG_FILL)
    new_max = jnp.maximum(old_max, jnp.max(scores, axis=2))
    weights = jnp.where(allowed[None], jnp.exp(scores - new_max[:, :, None]), 0.0)
    factor = jnp.exp(old_max - new_max)
    new_total = old_total * factor + jnp.sum(weights, axis=2)
    update = jnp.einsum(
        "hqk,kd->qhd",
        weights.astype(jnp.bfloat16),
        value_piece,
        preferred_element_type=jnp.float32,
    )
    new_accum = old_accum * factor.T[:, :, None] + update
    return (new_max, new_total, new_accum)


def swap_inner(piece_at, inner_index, inner_steps):
    arrived = [piece_at(inner_index)]
    for distance in range(1, inner_steps):
        route = [(i, (i + distance) % inner_steps) for i in range(inner_steps)]
        arrived.append(lax.ppermute(piece_at((inner_index + distance) % inner_steps), "inner", route))
    order = (inner_index - jnp.arange(inner_steps, dtype=jnp.int32)) % inner_steps
    return jnp.take(jnp.stack(arrived), order, axis=0)


def body(query_rows, key_matrix, value_matrix, unit_order, doc_lengths):
    inner_steps = lax.axis_size("inner")
    token_total = query_rows.shape[0]
    group_rows = inner_steps * token_total
    heads_here = QUERY_HEADS // inner_steps
    head_copies = inner_steps // KEY_VALUE_HEADS
    query_width = heads_here * HEAD_SIZE
    query_width = heads_here * HEAD_SIZE

    def widened_heads(score_matrix):
        return jnp.repeat(
            score_matrix.reshape(token_total, KEY_VALUE_HEADS, HEAD_SIZE), head_copies, axis=1
        )

    pairs = jnp.concatenate([widened_heads(key_matrix), widened_heads(value_matrix)], axis=2)
    inner_index = lax.axis_index("inner")
    pair_pieces = jnp.transpose(pairs, (1, 0, 2))
    own_pairs = swap_inner(
        lambda chunk: lax.dynamic_index_in_dim(pair_pieces, chunk, 0, keepdims=False),
        inner_index,
        inner_steps,
    )
    own_pairs = own_pairs.reshape(group_rows, 2 * HEAD_SIZE)
    outer_count = lax.axis_size("outer")
    outer_index = lax.axis_index("outer")
    received = [own_pairs]
    for distance in range(1, outer_count):
        route = [(i, (i + distance) % outer_count) for i in range(outer_count)]
        received.append(lax.ppermute(own_pairs, "outer", route))
    local_queries = lax.all_to_all(query_rows, "inner", split_axis=1, concat_axis=0, tiled=True)
    local_queries, early_order, early_lengths = lax.optimization_barrier(
        (local_queries, unit_order, doc_lengths)
    )
    shaped_queries = local_queries.reshape(group_rows, heads_here, HEAD_SIZE)
    unit_count = unit_order.shape[0]
    group_units = group_rows // UNIT_TOKENS
    group_begin = outer_index * group_units
    offsets = jnp.arange(UNIT_TOKENS, dtype=jnp.int32)
    early_ends = jnp.cumsum(early_lengths).astype(jnp.int32)

    outputs = []
    for query_unit in range(group_units):
        position_unit = early_order[group_begin + query_unit]
        query_pos = position_unit * UNIT_TOKENS + offsets
        query_start = jnp.max(
            jnp.where(early_ends[None, :] <= query_pos[:, None], early_ends[None, :], 0), axis=1
        )
        query_piece = shaped_queries[query_unit * UNIT_TOKENS : (query_unit + 1) * UNIT_TOKENS]

        def tile_at(carried, step, pair_piece):
            key_unit = position_unit - step
            key_pos = key_unit * UNIT_TOKENS + offsets
            return tile_update(
                carried,
                query_piece,
                pair_piece[:, :HEAD_SIZE],
                pair_piece[:, HEAD_SIZE:],
                query_pos,
                query_start,
                key_pos,
            )

        def visit(step, carried):
            key_row_unit = inverse[position_unit - step]
            source = (outer_index - key_row_unit // group_units) % outer_count
            key_row = (key_row_unit % group_units) * UNIT_TOKENS
            pair_piece = lax.switch(
                source,
                [
                    (lambda row, block=block: lax.dynamic_slice_in_dim(block, row, UNIT_TOKENS, 0))
                    for block in received
                ],
                key_row,
            )
            return tile_at(carried, step, pair_piece)

        running = (
            jnp.full((heads_here, UNIT_TOKENS), NEG_FILL, jnp.float32),
            jnp.zeros((heads_here, UNIT_TOKENS), jnp.float32),
            jnp.zeros((UNIT_TOKENS, heads_here, HEAD_SIZE), jnp.float32),
        )
        own_row = query_unit * UNIT_TOKENS
        running = tile_at(running, 0, own_pairs[own_row : own_row + UNIT_TOKENS])
        running, late_order, late_lengths = lax.optimization_barrier(
            (running, unit_order, doc_lengths)
        )
        inverse = jnp.zeros((unit_count,), jnp.int32).at[late_order].set(
            jnp.arange(unit_count, dtype=jnp.int32)
        )
        late_ends = jnp.cumsum(late_lengths).astype(jnp.int32)
        unit_start = jnp.max(
            jnp.where(late_ends <= late_order[group_begin + query_unit] * UNIT_TOKENS, late_ends, 0)
        )
        first_unit = unit_start // UNIT_TOKENS
        if group_units == 1:
            for distance in range(1, outer_count):
                key_unit = late_order[(outer_index - distance) % outer_count]
                needed = (key_unit >= first_unit) & (key_unit < position_unit)
                running = lax.cond(
                    needed,
                    lambda carried, key_unit=key_unit, block=received[distance]: tile_at(
                        carried, position_unit - key_unit, block
                    ),
                    lambda carried: carried,
                    running,
                )
        else:
            running = lax.fori_loop(1, position_unit - first_unit + 1, visit, running)
        _, totals, accumulated = running
        outputs.append((accumulated, totals.T))
    accumulated = jnp.concatenate([part[0] for part in outputs], axis=0)
    totals = jnp.concatenate([part[1] for part in outputs], axis=0)

    def finished(chunk):
        begin = chunk * token_total
        rows = lax.dynamic_slice_in_dim(accumulated, begin, token_total, 0)
        sums = lax.dynamic_slice_in_dim(totals, begin, token_total, 0)
        return (rows / sums[:, :, None]).reshape(token_total, query_width).astype(jnp.bfloat16)

    placed = swap_inner(finished, inner_index, inner_steps)
    return jnp.transpose(placed, (1, 0, 2)).reshape(token_total, inner_steps * query_width)


def solution(mesh):
    placed = (
        P(("outer", "inner"), None),
        P(("outer", "inner"), None),
        P(("outer", "inner"), None),
        P(),
        P(),
    )
    return jax.shard_map(
        body, mesh=mesh, in_specs=placed, out_specs=P(("outer", "inner"), None), check_vma=False
    )
```

```python
import jax
import jax.numpy as jnp
from jax import lax
from jax.sharding import PartitionSpec as P

QUERY_HEADS = 32
KEY_VALUE_HEADS = 4
HEAD_SIZE = 128
UNIT_TOKENS = 512


NEG_FILL = -1e30


def tile_update(running, query_piece, key_piece, value_piece, query_pos, query_start, key_pos):
    old_max, old_total, old_accum = running
    tile_rows, heads_here, _ = query_piece.shape
    allowed = (key_pos[None, :] >= query_start[:, None]) & (key_pos[None, :] <= query_pos[:, None])
    scores = jnp.einsum(
        "qhd,kd->hqk", query_piece, key_piece, preferred_element_type=jnp.float32
    ) * HEAD_SIZE ** (-0.5)
    scores = jnp.where(allowed[None], scores, NEG_FILL)
    new_max = jnp.maximum(old_max, jnp.max(scores, axis=2))
    weights = jnp.where(allowed[None], jnp.exp(scores - new_max[:, :, None]), 0.0)
    factor = jnp.exp(old_max - new_max)
    new_total = old_total * factor + jnp.sum(weights, axis=2)
    update = jnp.einsum(
        "hqk,kd->qhd",
        weights.astype(jnp.bfloat16),
        value_piece,
        preferred_element_type=jnp.float32,
    )
    new_accum = old_accum * factor.T[:, :, None] + update
    return (new_max, new_total, new_accum)


def swap_inner(piece_at, inner_index, inner_steps):
    arrived = [piece_at(inner_index)]
    for distance in range(1, inner_steps):
        route = [(i, (i + distance) % inner_steps) for i in range(inner_steps)]
        arrived.append(lax.ppermute(piece_at((inner_index + distance) % inner_steps), "inner", route))
    order = (inner_index - jnp.arange(inner_steps, dtype=jnp.int32)) % inner_steps
    return [
        lax.dynamic_index_in_dim(jnp.stack(arrived), order[chunk], 0, keepdims=False)
        for chunk in range(inner_steps)
    ]


def place_inner(piece_at, inner_index, inner_steps, width):
    arrived = [piece_at(inner_index)]
    for distance in range(1, inner_steps):
        route = [(i, (i + distance) % inner_steps) for i in range(inner_steps)]
        arrived.append(lax.ppermute(piece_at((inner_index + distance) % inner_steps), "inner", route))
    result = jnp.zeros((arrived[0].shape[0], inner_steps * width), arrived[0].dtype)
    for distance, piece in enumerate(arrived):
        column = ((inner_index - distance) % inner_steps) * width
        result = lax.dynamic_update_slice_in_dim(result, piece, column, 1)
    return result


def body(query_rows, key_matrix, value_matrix, unit_order, doc_lengths):
    inner_steps = lax.axis_size("inner")
    token_total = query_rows.shape[0]
    group_rows = inner_steps * token_total
    heads_here = QUERY_HEADS // inner_steps
    head_copies = inner_steps // KEY_VALUE_HEADS
    query_width = heads_here * HEAD_SIZE
    query_width = heads_here * HEAD_SIZE

    inner_index = lax.axis_index("inner")

    def pair_piece_for(chunk):
        column = (chunk // head_copies) * HEAD_SIZE
        return jnp.concatenate(
            [
                lax.dynamic_slice_in_dim(key_matrix, column, HEAD_SIZE, 1),
                lax.dynamic_slice_in_dim(value_matrix, column, HEAD_SIZE, 1),
            ],
            axis=1,
        )

    own_pairs = jnp.stack(swap_inner(pair_piece_for, inner_index, inner_steps))
    own_pairs = own_pairs.reshape(group_rows, 2 * HEAD_SIZE)
    outer_count = lax.axis_size("outer")
    outer_index = lax.axis_index("outer")
    received = [own_pairs]
    for distance in range(1, outer_count):
        route = [(i, (i + distance) % outer_count) for i in range(outer_count)]
        received.append(lax.ppermute(own_pairs, "outer", route))
    local_queries = lax.all_to_all(query_rows, "inner", split_axis=1, concat_axis=0, tiled=True)
    local_queries, early_order, early_lengths = lax.optimization_barrier(
        (local_queries, unit_order, doc_lengths)
    )
    shaped_queries = local_queries.reshape(group_rows, heads_here, HEAD_SIZE)
    unit_count = unit_order.shape[0]
    group_units = group_rows // UNIT_TOKENS
    group_begin = outer_index * group_units
    offsets = jnp.arange(UNIT_TOKENS, dtype=jnp.int32)
    early_ends = jnp.cumsum(early_lengths).astype(jnp.int32)

    outputs = []
    for query_unit in range(group_units):
        position_unit = early_order[group_begin + query_unit]
        query_pos = position_unit * UNIT_TOKENS + offsets
        query_start = jnp.max(
            jnp.where(early_ends[None, :] <= query_pos[:, None], early_ends[None, :], 0), axis=1
        )
        query_piece = shaped_queries[query_unit * UNIT_TOKENS : (query_unit + 1) * UNIT_TOKENS]

        def tile_at(carried, step, pair_piece):
            key_unit = position_unit - step
            key_pos = key_unit * UNIT_TOKENS + offsets
            return tile_update(
                carried,
                query_piece,
                pair_piece[:, :HEAD_SIZE],
                pair_piece[:, HEAD_SIZE:],
                query_pos,
                query_start,
                key_pos,
            )

        def visit(step, carried):
            key_row_unit = inverse[position_unit - step]
            source = (outer_index - key_row_unit // group_units) % outer_count
            key_row = (key_row_unit % group_units) * UNIT_TOKENS
            pair_piece = lax.switch(
                source,
                [
                    (lambda row, block=block: lax.dynamic_slice_in_dim(block, row, UNIT_TOKENS, 0))
                    for block in received
                ],
                key_row,
            )
            return tile_at(carried, step, pair_piece)

        running = (
            jnp.full((heads_here, UNIT_TOKENS), NEG_FILL, jnp.float32),
            jnp.zeros((heads_here, UNIT_TOKENS), jnp.float32),
            jnp.zeros((UNIT_TOKENS, heads_here, HEAD_SIZE), jnp.float32),
        )
        own_row = query_unit * UNIT_TOKENS
        running = tile_at(running, 0, own_pairs[own_row : own_row + UNIT_TOKENS])
        running, late_order, late_lengths = lax.optimization_barrier(
            (running, unit_order, doc_lengths)
        )
        inverse = jnp.zeros((unit_count,), jnp.int32).at[late_order].set(
            jnp.arange(unit_count, dtype=jnp.int32)
        )
        late_ends = jnp.cumsum(late_lengths).astype(jnp.int32)
        unit_start = jnp.max(
            jnp.where(late_ends <= late_order[group_begin + query_unit] * UNIT_TOKENS, late_ends, 0)
        )
        first_unit = unit_start // UNIT_TOKENS
        _, totals, accumulated = lax.fori_loop(
            1, position_unit - first_unit + 1, visit, running
        )
        outputs.append((accumulated, totals.T))
    accumulated = jnp.concatenate([part[0] for part in outputs], axis=0)
    totals = jnp.concatenate([part[1] for part in outputs], axis=0)

    def finished(chunk):
        begin = chunk * token_total
        rows = lax.dynamic_slice_in_dim(accumulated, begin, token_total, 0)
        sums = lax.dynamic_slice_in_dim(totals, begin, token_total, 0)
        return (rows / sums[:, :, None]).reshape(token_total, query_width).astype(jnp.bfloat16)

    return place_inner(finished, inner_index, inner_steps, query_width)


def solution(mesh):
    placed = (
        P(("outer", "inner"), None),
        P(("outer", "inner"), None),
        P(("outer", "inner"), None),
        P(),
        P(),
    )
    return jax.shard_map(
        body, mesh=mesh, in_specs=placed, out_specs=P(("outer", "inner"), None), check_vma=False
    )
```

```python
import jax
import jax.numpy as jnp
from jax import lax
from jax.sharding import PartitionSpec as P

QUERY_HEADS = 32
KEY_VALUE_HEADS = 4
HEAD_SIZE = 128
UNIT_TOKENS = 512


NEG_FILL = -1e30


def tile_update(running, query_piece, key_piece, value_piece, query_pos, query_start, key_pos):
    old_max, old_total, old_accum = running
    tile_rows, heads_here, _ = query_piece.shape
    allowed = (key_pos[None, :] >= query_start[:, None]) & (key_pos[None, :] <= query_pos[:, None])
    scores = jnp.einsum(
        "qhd,kd->hqk", query_piece, key_piece, preferred_element_type=jnp.float32
    ) * HEAD_SIZE ** (-0.5)
    scores = jnp.where(allowed[None], scores, NEG_FILL)
    new_max = jnp.maximum(old_max, jnp.max(scores, axis=2))
    weights = jnp.where(allowed[None], jnp.exp(scores - new_max[:, :, None]), 0.0)
    factor = jnp.exp(old_max - new_max)
    new_total = old_total * factor + jnp.sum(weights, axis=2)
    update = jnp.einsum(
        "hqk,kd->qhd",
        weights.astype(jnp.bfloat16),
        value_piece,
        preferred_element_type=jnp.float32,
    )
    new_accum = old_accum * factor.T[:, :, None] + update
    return (new_max, new_total, new_accum)


def swap_inner(piece_at, inner_index, inner_steps):
    arrived = [piece_at(inner_index)]
    for distance in range(1, inner_steps):
        route = [(i, (i + distance) % inner_steps) for i in range(inner_steps)]
        arrived.append(lax.ppermute(piece_at((inner_index + distance) % inner_steps), "inner", route))
    order = (inner_index - jnp.arange(inner_steps, dtype=jnp.int32)) % inner_steps
    return jnp.take(jnp.stack(arrived), order, axis=0)


def body(query_rows, key_matrix, value_matrix, unit_order, doc_lengths):
    inner_steps = lax.axis_size("inner")
    token_total = query_rows.shape[0]
    group_rows = inner_steps * token_total
    heads_here = QUERY_HEADS // inner_steps
    head_copies = inner_steps // KEY_VALUE_HEADS
    query_width = heads_here * HEAD_SIZE
    query_width = heads_here * HEAD_SIZE

    def widened_heads(score_matrix):
        return jnp.repeat(
            score_matrix.reshape(token_total, KEY_VALUE_HEADS, HEAD_SIZE), head_copies, axis=1
        )

    pairs = jnp.concatenate([widened_heads(key_matrix), widened_heads(value_matrix)], axis=2)
    inner_index = lax.axis_index("inner")
    pair_pieces = jnp.transpose(pairs, (1, 0, 2))
    own_pairs = swap_inner(
        lambda chunk: lax.dynamic_index_in_dim(pair_pieces, chunk, 0, keepdims=False),
        inner_index,
        inner_steps,
    )
    own_pairs = own_pairs.reshape(group_rows, 2 * HEAD_SIZE)
    outer_count = lax.axis_size("outer")
    outer_index = lax.axis_index("outer")
    received = [own_pairs]
    for distance in range(1, outer_count):
        route = [(i, (i + distance) % outer_count) for i in range(outer_count)]
        received.append(lax.ppermute(own_pairs, "outer", route))
    local_queries = lax.all_to_all(query_rows, "inner", split_axis=1, concat_axis=0, tiled=True)
    local_queries, early_order, early_lengths = lax.optimization_barrier(
        (local_queries, unit_order, doc_lengths)
    )
    shaped_queries = local_queries.reshape(group_rows, heads_here, HEAD_SIZE)
    unit_count = unit_order.shape[0]
    group_units = group_rows // UNIT_TOKENS
    group_begin = outer_index * group_units
    offsets = jnp.arange(UNIT_TOKENS, dtype=jnp.int32)
    early_ends = jnp.cumsum(early_lengths).astype(jnp.int32)

    outputs = []
    for query_unit in range(group_units):
        position_unit = early_order[group_begin + query_unit]
        query_pos = position_unit * UNIT_TOKENS + offsets
        query_start = jnp.max(
            jnp.where(early_ends[None, :] <= query_pos[:, None], early_ends[None, :], 0), axis=1
        )
        query_piece = shaped_queries[query_unit * UNIT_TOKENS : (query_unit + 1) * UNIT_TOKENS]

        def tile_at(carried, step, pair_piece):
            key_unit = position_unit - step
            key_pos = key_unit * UNIT_TOKENS + offsets
            return tile_update(
                carried,
                query_piece,
                pair_piece[:, :HEAD_SIZE],
                pair_piece[:, HEAD_SIZE:],
                query_pos,
                query_start,
                key_pos,
            )

        half_rows = UNIT_TOKENS // 2

        def half_tile(carried, key_unit, pair_piece):
            key_pos = key_unit * UNIT_TOKENS + offsets
            part = tile_update(
                (carried[0][:, :half_rows], carried[1][:, :half_rows], carried[2][:half_rows]),
                query_piece[:half_rows],
                pair_piece[:, :HEAD_SIZE],
                pair_piece[:, HEAD_SIZE:],
                query_pos[:half_rows],
                query_start[:half_rows],
                key_pos,
            )
            return (
                lax.dynamic_update_slice_in_dim(carried[0], part[0], 0, 1),
                lax.dynamic_update_slice_in_dim(carried[1], part[1], 0, 1),
                lax.dynamic_update_slice_in_dim(carried[2], part[2], 0, 0),
            )

        def visit(step, carried):
            key_unit = position_unit - step
            key_row_unit = inverse[key_unit]
            source = (outer_index - key_row_unit // group_units) % outer_count
            key_row = (key_row_unit % group_units) * UNIT_TOKENS
            pair_piece = lax.switch(
                source,
                [
                    (lambda row, block=block: lax.dynamic_slice_in_dim(block, row, UNIT_TOKENS, 0))
                    for block in received
                ],
                key_row,
            )
            upper_needed = upper_start <= key_unit * UNIT_TOKENS + UNIT_TOKENS - 1
            return lax.cond(
                upper_needed,
                lambda c: tile_at(c, step, pair_piece),
                lambda c: half_tile(c, key_unit, pair_piece),
                carried,
            )

        running = (
            jnp.full((heads_here, UNIT_TOKENS), NEG_FILL, jnp.float32),
            jnp.zeros((heads_here, UNIT_TOKENS), jnp.float32),
            jnp.zeros((UNIT_TOKENS, heads_here, HEAD_SIZE), jnp.float32),
        )
        own_row = query_unit * UNIT_TOKENS
        running = tile_at(running, 0, own_pairs[own_row : own_row + UNIT_TOKENS])
        running, late_order, late_lengths = lax.optimization_barrier(
            (running, unit_order, doc_lengths)
        )
        inverse = jnp.zeros((unit_count,), jnp.int32).at[late_order].set(
            jnp.arange(unit_count, dtype=jnp.int32)
        )
        late_ends = jnp.cumsum(late_lengths).astype(jnp.int32)
        unit_start = jnp.max(
            jnp.where(late_ends <= late_order[group_begin + query_unit] * UNIT_TOKENS, late_ends, 0)
        )
        first_unit = unit_start // UNIT_TOKENS
        upper_pos = late_order[group_begin + query_unit] * UNIT_TOKENS + UNIT_TOKENS // 2
        upper_start = jnp.max(jnp.where(late_ends <= upper_pos, late_ends, 0))
        _, totals, accumulated = lax.fori_loop(
            1, position_unit - first_unit + 1, visit, running
        )
        outputs.append((accumulated, totals.T))
    accumulated = jnp.concatenate([part[0] for part in outputs], axis=0)
    totals = jnp.concatenate([part[1] for part in outputs], axis=0)

    def finished(chunk):
        begin = chunk * token_total
        rows = lax.dynamic_slice_in_dim(accumulated, begin, token_total, 0)
        sums = lax.dynamic_slice_in_dim(totals, begin, token_total, 0)
        return (rows / sums[:, :, None]).reshape(token_total, query_width).astype(jnp.bfloat16)

    placed = swap_inner(finished, inner_index, inner_steps)
    return jnp.transpose(placed, (1, 0, 2)).reshape(token_total, inner_steps * query_width)


def solution(mesh):
    placed = (
        P(("outer", "inner"), None),
        P(("outer", "inner"), None),
        P(("outer", "inner"), None),
        P(),
        P(),
    )
    return jax.shard_map(
        body, mesh=mesh, in_specs=placed, out_specs=P(("outer", "inner"), None), check_vma=False
    )
```

```python
import jax
import jax.numpy as jnp
from jax import lax
from jax.sharding import PartitionSpec as P

QUERY_HEADS = 32
KEY_VALUE_HEADS = 4
HEAD_SIZE = 128
UNIT_TOKENS = 512


NEG_FILL = -1e30


def tile_update(running, query_piece, key_piece, value_piece, query_pos, query_start, key_pos):
    old_max, old_total, old_accum = running
    tile_rows, heads_here, _ = query_piece.shape
    allowed = (key_pos[None, :] >= query_start[:, None]) & (key_pos[None, :] <= query_pos[:, None])
    scores = jnp.einsum(
        "qhd,kd->hqk", query_piece, key_piece, preferred_element_type=jnp.float32
    ) * HEAD_SIZE ** (-0.5)
    scores = jnp.where(allowed[None], scores, NEG_FILL)
    new_max = jnp.maximum(old_max, jnp.max(scores, axis=2))
    weights = jnp.where(allowed[None], jnp.exp(scores - new_max[:, :, None]), 0.0)
    factor = jnp.exp(old_max - new_max)
    new_total = old_total * factor + jnp.sum(weights, axis=2)
    update = jnp.einsum(
        "hqk,kd->qhd",
        weights.astype(jnp.bfloat16),
        value_piece,
        preferred_element_type=jnp.float32,
    )
    new_accum = old_accum * factor.T[:, :, None] + update
    return (new_max, new_total, new_accum)


def swap_inner(piece_at, inner_index, inner_steps):
    arrived = [piece_at(inner_index)]
    for distance in range(1, inner_steps):
        route = [(i, (i + distance) % inner_steps) for i in range(inner_steps)]
        arrived.append(lax.ppermute(piece_at((inner_index + distance) % inner_steps), "inner", route))
    order = (inner_index - jnp.arange(inner_steps, dtype=jnp.int32)) % inner_steps
    return jnp.take(jnp.stack(arrived), order, axis=0)


def body(query_rows, key_matrix, value_matrix, unit_order, doc_lengths):
    inner_steps = lax.axis_size("inner")
    token_total = query_rows.shape[0]
    group_rows = inner_steps * token_total
    heads_here = QUERY_HEADS // inner_steps
    head_copies = inner_steps // KEY_VALUE_HEADS
    query_width = heads_here * HEAD_SIZE
    query_width = heads_here * HEAD_SIZE

    def widened_heads(score_matrix):
        return jnp.repeat(
            score_matrix.reshape(token_total, KEY_VALUE_HEADS, HEAD_SIZE), head_copies, axis=1
        )

    pairs = jnp.concatenate([widened_heads(key_matrix), widened_heads(value_matrix)], axis=2)
    inner_index = lax.axis_index("inner")
    pair_pieces = jnp.transpose(pairs, (1, 0, 2))
    own_pairs = swap_inner(
        lambda chunk: lax.dynamic_index_in_dim(pair_pieces, chunk, 0, keepdims=False),
        inner_index,
        inner_steps,
    )
    own_pairs = own_pairs.reshape(group_rows, 2 * HEAD_SIZE)
    outer_count = lax.axis_size("outer")
    outer_index = lax.axis_index("outer")
    received = [own_pairs]
    for distance in range(1, outer_count):
        route = [(i, (i + distance) % outer_count) for i in range(outer_count)]
        received.append(lax.ppermute(own_pairs, "outer", route))
    local_queries = lax.all_to_all(query_rows, "inner", split_axis=1, concat_axis=0, tiled=True)
    local_queries, early_order, early_lengths = lax.optimization_barrier(
        (local_queries, unit_order, doc_lengths)
    )
    shaped_queries = local_queries.reshape(group_rows, heads_here, HEAD_SIZE)
    unit_count = unit_order.shape[0]
    group_units = group_rows // UNIT_TOKENS
    group_begin = outer_index * group_units
    offsets = jnp.arange(UNIT_TOKENS, dtype=jnp.int32)
    early_ends = jnp.cumsum(early_lengths).astype(jnp.int32)

    splits = 2 if heads_here % 2 == 0 else 1
    split_heads = heads_here // splits
    outputs = [[] for _ in range(splits)]
    for query_unit in range(group_units):
        position_unit = early_order[group_begin + query_unit]
        query_pos = position_unit * UNIT_TOKENS + offsets
        query_start = jnp.max(
            jnp.where(early_ends[None, :] <= query_pos[:, None], early_ends[None, :], 0), axis=1
        )
        unit_queries = shaped_queries[query_unit * UNIT_TOKENS : (query_unit + 1) * UNIT_TOKENS]

        def tile_at(carried, step, pair_piece, query_piece):
            key_unit = position_unit - step
            key_pos = key_unit * UNIT_TOKENS + offsets
            return tile_update(
                carried,
                query_piece,
                pair_piece[:, :HEAD_SIZE],
                pair_piece[:, HEAD_SIZE:],
                query_pos,
                query_start,
                key_pos,
            )

        own_row = query_unit * UNIT_TOKENS
        states = []
        for part in range(splits):
            running = (
                jnp.full((split_heads, UNIT_TOKENS), NEG_FILL, jnp.float32),
                jnp.zeros((split_heads, UNIT_TOKENS), jnp.float32),
                jnp.zeros((UNIT_TOKENS, split_heads, HEAD_SIZE), jnp.float32),
            )
            query_piece = unit_queries[:, part * split_heads : (part + 1) * split_heads]
            states.append(
                tile_at(running, 0, own_pairs[own_row : own_row + UNIT_TOKENS], query_piece)
            )
        states, late_order, late_lengths = lax.optimization_barrier(
            (states, unit_order, doc_lengths)
        )
        inverse = jnp.zeros((unit_count,), jnp.int32).at[late_order].set(
            jnp.arange(unit_count, dtype=jnp.int32)
        )
        late_ends = jnp.cumsum(late_lengths).astype(jnp.int32)
        unit_start = jnp.max(
            jnp.where(late_ends <= late_order[group_begin + query_unit] * UNIT_TOKENS, late_ends, 0)
        )
        first_unit = unit_start // UNIT_TOKENS

        for part in range(splits):
            query_piece = unit_queries[:, part * split_heads : (part + 1) * split_heads]

            def visit(step, carried, query_piece=query_piece):
                key_row_unit = inverse[position_unit - step]
                source = (outer_index - key_row_unit // group_units) % outer_count
                key_row = (key_row_unit % group_units) * UNIT_TOKENS
                pair_piece = lax.switch(
                    source,
                    [
                        (
                            lambda row, block=block: lax.dynamic_slice_in_dim(
                                block, row, UNIT_TOKENS, 0
                            )
                        )
                        for block in received
                    ],
                    key_row,
                )
                return tile_at(carried, step, pair_piece, query_piece)

            _, totals, accumulated = lax.fori_loop(
                1, position_unit - first_unit + 1, visit, states[part]
            )
            outputs[part].append((accumulated, totals.T))

    split_width = split_heads * HEAD_SIZE
    placed_parts = []
    for part in range(splits):
        accumulated = jnp.concatenate([piece[0] for piece in outputs[part]], axis=0)
        totals = jnp.concatenate([piece[1] for piece in outputs[part]], axis=0)

        def finished(chunk, accumulated=accumulated, totals=totals):
            begin = chunk * token_total
            rows = lax.dynamic_slice_in_dim(accumulated, begin, token_total, 0)
            sums = lax.dynamic_slice_in_dim(totals, begin, token_total, 0)
            return (rows / sums[:, :, None]).reshape(token_total, split_width).astype(jnp.bfloat16)

        placed_parts.append(swap_inner(finished, inner_index, inner_steps))
    placed = jnp.concatenate(placed_parts, axis=2) if splits > 1 else placed_parts[0]
    return jnp.transpose(placed, (1, 0, 2)).reshape(token_total, inner_steps * query_width)


def solution(mesh):
    placed = (
        P(("outer", "inner"), None),
        P(("outer", "inner"), None),
        P(("outer", "inner"), None),
        P(),
        P(),
    )
    return jax.shard_map(
        body, mesh=mesh, in_specs=placed, out_specs=P(("outer", "inner"), None), check_vma=False
    )
```

```python
import jax
import jax.numpy as jnp
from jax import lax
from jax.sharding import PartitionSpec as P

QUERY_HEADS = 32
KEY_VALUE_HEADS = 4
HEAD_SIZE = 128
UNIT_TOKENS = 512


NEG_FILL = -1e30


def tile_update(running, query_piece, key_piece, value_piece, query_pos, query_start, key_pos):
    old_max, old_total, old_accum = running
    tile_rows, heads_here, _ = query_piece.shape
    allowed = (key_pos[None, :] >= query_start[:, None]) & (key_pos[None, :] <= query_pos[:, None])
    scores = jnp.einsum(
        "qhd,kd->hqk", query_piece, key_piece, preferred_element_type=jnp.float32
    ) * HEAD_SIZE ** (-0.5)
    scores = jnp.where(allowed[None], scores, NEG_FILL)
    new_max = jnp.maximum(old_max, jnp.max(scores, axis=2))
    weights = jnp.where(allowed[None], jnp.exp(scores - new_max[:, :, None]), 0.0)
    factor = jnp.exp(old_max - new_max)
    new_total = old_total * factor + jnp.sum(weights, axis=2)
    update = jnp.einsum(
        "hqk,kd->qhd",
        weights.astype(jnp.bfloat16),
        value_piece,
        preferred_element_type=jnp.float32,
    )
    new_accum = old_accum * factor.T[:, :, None] + update
    return (new_max, new_total, new_accum)


def swap_inner(piece_at, inner_index, inner_steps):
    arrived = [piece_at(inner_index)]
    for distance in range(1, inner_steps):
        route = [(i, (i + distance) % inner_steps) for i in range(inner_steps)]
        arrived.append(lax.ppermute(piece_at((inner_index + distance) % inner_steps), "inner", route))
    order = (inner_index - jnp.arange(inner_steps, dtype=jnp.int32)) % inner_steps
    return jnp.take(jnp.stack(arrived), order, axis=0)


def place_inner(piece_at, inner_index, inner_steps, width):
    arrived = [piece_at(inner_index)]
    for distance in range(1, inner_steps):
        route = [(i, (i + distance) % inner_steps) for i in range(inner_steps)]
        arrived.append(lax.ppermute(piece_at((inner_index + distance) % inner_steps), "inner", route))
    result = jnp.zeros((arrived[0].shape[0], inner_steps * width), arrived[0].dtype)
    for distance, piece in enumerate(arrived):
        column = ((inner_index - distance) % inner_steps) * width
        result = lax.dynamic_update_slice_in_dim(result, piece, column, 1)
    return result


def body(query_rows, key_matrix, value_matrix, unit_order, doc_lengths):
    inner_steps = lax.axis_size("inner")
    token_total = query_rows.shape[0]
    group_rows = inner_steps * token_total
    heads_here = QUERY_HEADS // inner_steps
    head_copies = inner_steps // KEY_VALUE_HEADS
    query_width = heads_here * HEAD_SIZE
    query_width = heads_here * HEAD_SIZE

    def widened_heads(score_matrix):
        return jnp.repeat(
            score_matrix.reshape(token_total, KEY_VALUE_HEADS, HEAD_SIZE), head_copies, axis=1
        )

    pairs = jnp.concatenate([widened_heads(key_matrix), widened_heads(value_matrix)], axis=2)
    inner_index = lax.axis_index("inner")
    pair_pieces = jnp.transpose(pairs, (1, 0, 2))
    own_pairs = swap_inner(
        lambda chunk: lax.dynamic_index_in_dim(pair_pieces, chunk, 0, keepdims=False),
        inner_index,
        inner_steps,
    )
    own_pairs = own_pairs.reshape(group_rows, 2 * HEAD_SIZE)
    outer_count = lax.axis_size("outer")
    outer_index = lax.axis_index("outer")
    received = [own_pairs]
    for distance in range(1, outer_count):
        route = [(i, (i + distance) % outer_count) for i in range(outer_count)]
        received.append(lax.ppermute(own_pairs, "outer", route))
    local_queries = lax.all_to_all(query_rows, "inner", split_axis=1, concat_axis=0, tiled=True)
    local_queries, early_order, early_lengths = lax.optimization_barrier(
        (local_queries, unit_order, doc_lengths)
    )
    shaped_queries = local_queries.reshape(group_rows, heads_here, HEAD_SIZE)
    unit_count = unit_order.shape[0]
    group_units = group_rows // UNIT_TOKENS
    group_begin = outer_index * group_units
    offsets = jnp.arange(UNIT_TOKENS, dtype=jnp.int32)
    early_ends = jnp.cumsum(early_lengths).astype(jnp.int32)

    outputs = []
    for query_unit in range(group_units):
        position_unit = early_order[group_begin + query_unit]
        query_pos = position_unit * UNIT_TOKENS + offsets
        query_start = jnp.max(
            jnp.where(early_ends[None, :] <= query_pos[:, None], early_ends[None, :], 0), axis=1
        )
        query_piece = shaped_queries[query_unit * UNIT_TOKENS : (query_unit + 1) * UNIT_TOKENS]

        def tile_at(carried, step, pair_piece):
            key_unit = position_unit - step
            key_pos = key_unit * UNIT_TOKENS + offsets
            return tile_update(
                carried,
                query_piece,
                pair_piece[:, :HEAD_SIZE],
                pair_piece[:, HEAD_SIZE:],
                query_pos,
                query_start,
                key_pos,
            )

        def visit(step, carried):
            key_row_unit = inverse[position_unit - step]
            source = (outer_index - key_row_unit // group_units) % outer_count
            key_row = (key_row_unit % group_units) * UNIT_TOKENS
            pair_piece = lax.switch(
                source,
                [
                    (lambda row, block=block: lax.dynamic_slice_in_dim(block, row, UNIT_TOKENS, 0))
                    for block in received
                ],
                key_row,
            )
            return tile_at(carried, step, pair_piece)

        running = (
            jnp.full((heads_here, UNIT_TOKENS), NEG_FILL, jnp.float32),
            jnp.zeros((heads_here, UNIT_TOKENS), jnp.float32),
            jnp.zeros((UNIT_TOKENS, heads_here, HEAD_SIZE), jnp.float32),
        )
        own_row = query_unit * UNIT_TOKENS
        running = tile_at(running, 0, own_pairs[own_row : own_row + UNIT_TOKENS])
        running, late_order, late_lengths = lax.optimization_barrier(
            (running, unit_order, doc_lengths)
        )
        inverse = jnp.zeros((unit_count,), jnp.int32).at[late_order].set(
            jnp.arange(unit_count, dtype=jnp.int32)
        )
        late_ends = jnp.cumsum(late_lengths).astype(jnp.int32)
        unit_start = jnp.max(
            jnp.where(late_ends <= late_order[group_begin + query_unit] * UNIT_TOKENS, late_ends, 0)
        )
        first_unit = unit_start // UNIT_TOKENS
        _, totals, accumulated = lax.fori_loop(
            1, position_unit - first_unit + 1, visit, running
        )
        outputs.append((accumulated, totals.T))
    accumulated = jnp.concatenate([part[0] for part in outputs], axis=0)
    totals = jnp.concatenate([part[1] for part in outputs], axis=0)

    def finished(chunk):
        begin = chunk * token_total
        rows = lax.dynamic_slice_in_dim(accumulated, begin, token_total, 0)
        sums = lax.dynamic_slice_in_dim(totals, begin, token_total, 0)
        return (rows / sums[:, :, None]).reshape(token_total, query_width).astype(jnp.bfloat16)

    return place_inner(finished, inner_index, inner_steps, query_width)


def solution(mesh):
    placed = (
        P(("outer", "inner"), None),
        P(("outer", "inner"), None),
        P(("outer", "inner"), None),
        P(),
        P(),
    )
    return jax.shard_map(
        body, mesh=mesh, in_specs=placed, out_specs=P(("outer", "inner"), None), check_vma=False
    )
```

```python
import jax
import jax.numpy as jnp
from jax import lax
from jax.sharding import PartitionSpec as P

QUERY_HEADS = 32
KEY_VALUE_HEADS = 4
HEAD_SIZE = 128
UNIT_TOKENS = 512


NEG_FILL = -1e30


def tile_update(running, query_piece, key_piece, value_piece, query_pos, query_start, key_pos):
    old_max, old_total, old_accum = running
    tile_rows, heads_here, _ = query_piece.shape
    allowed = (key_pos[None, :] >= query_start[:, None]) & (key_pos[None, :] <= query_pos[:, None])
    scores = jnp.einsum(
        "qhd,kd->hqk", query_piece, key_piece, preferred_element_type=jnp.float32
    ) * HEAD_SIZE ** (-0.5)
    scores = jnp.where(allowed[None], scores, NEG_FILL)
    new_max = jnp.maximum(old_max, jnp.max(scores, axis=2))
    weights = jnp.where(allowed[None], jnp.exp(scores - new_max[:, :, None]), 0.0)
    factor = jnp.exp(old_max - new_max)
    new_total = old_total * factor + jnp.sum(weights, axis=2)
    update = jnp.einsum(
        "hqk,kd->qhd",
        weights.astype(jnp.bfloat16),
        value_piece,
        preferred_element_type=jnp.float32,
    )
    new_accum = old_accum * factor.T[:, :, None] + update
    return (new_max, new_total, new_accum)


def swap_inner(piece_at, inner_index, inner_steps):
    arrived = [piece_at(inner_index)]
    for distance in range(1, inner_steps):
        route = [(i, (i + distance) % inner_steps) for i in range(inner_steps)]
        arrived.append(lax.ppermute(piece_at((inner_index + distance) % inner_steps), "inner", route))
    order = (inner_index - jnp.arange(inner_steps, dtype=jnp.int32)) % inner_steps
    return jnp.take(jnp.stack(arrived), order, axis=0)


def place_inner(piece_at, inner_index, inner_steps, width):
    arrived = [piece_at(inner_index)]
    for distance in range(1, inner_steps):
        route = [(i, (i + distance) % inner_steps) for i in range(inner_steps)]
        arrived.append(lax.ppermute(piece_at((inner_index + distance) % inner_steps), "inner", route))
    result = jnp.zeros((arrived[0].shape[0], inner_steps * width), arrived[0].dtype)
    for distance, piece in enumerate(arrived):
        column = ((inner_index - distance) % inner_steps) * width
        result = lax.dynamic_update_slice_in_dim(result, piece, column, 1)
    return result


def body(query_rows, key_matrix, value_matrix, unit_order, doc_lengths):
    inner_steps = lax.axis_size("inner")
    token_total = query_rows.shape[0]
    group_rows = inner_steps * token_total
    heads_here = QUERY_HEADS // inner_steps
    head_copies = inner_steps // KEY_VALUE_HEADS
    query_width = heads_here * HEAD_SIZE
    query_width = heads_here * HEAD_SIZE

    def widened_heads(score_matrix):
        return jnp.repeat(
            score_matrix.reshape(token_total, KEY_VALUE_HEADS, HEAD_SIZE), head_copies, axis=1
        )

    pairs = jnp.concatenate([widened_heads(key_matrix), widened_heads(value_matrix)], axis=2)
    inner_index = lax.axis_index("inner")
    pair_pieces = jnp.transpose(pairs, (1, 0, 2))
    own_pairs = swap_inner(
        lambda chunk: lax.dynamic_index_in_dim(pair_pieces, chunk, 0, keepdims=False),
        inner_index,
        inner_steps,
    )
    own_pairs = own_pairs.reshape(group_rows, 2 * HEAD_SIZE)
    outer_count = lax.axis_size("outer")
    outer_index = lax.axis_index("outer")
    received = [own_pairs]
    for distance in range(1, outer_count):
        route = [(i, (i + distance) % outer_count) for i in range(outer_count)]
        received.append(lax.ppermute(own_pairs, "outer", route))
    local_queries = lax.all_to_all(query_rows, "inner", split_axis=1, concat_axis=0, tiled=True)
    local_queries, early_order, early_lengths = lax.optimization_barrier(
        (local_queries, unit_order, doc_lengths)
    )
    shaped_queries = local_queries.reshape(group_rows, heads_here, HEAD_SIZE)
    unit_count = unit_order.shape[0]
    group_units = group_rows // UNIT_TOKENS
    group_begin = outer_index * group_units
    offsets = jnp.arange(UNIT_TOKENS, dtype=jnp.int32)
    early_ends = jnp.cumsum(early_lengths).astype(jnp.int32)

    outputs = []
    for query_unit in range(group_units):
        position_unit = early_order[group_begin + query_unit]
        query_pos = position_unit * UNIT_TOKENS + offsets
        query_start = jnp.max(
            jnp.where(early_ends[None, :] <= query_pos[:, None], early_ends[None, :], 0), axis=1
        )
        query_piece = shaped_queries[query_unit * UNIT_TOKENS : (query_unit + 1) * UNIT_TOKENS]

        def tile_at(carried, step, pair_piece):
            key_unit = position_unit - step
            key_pos = key_unit * UNIT_TOKENS + offsets
            return tile_update(
                carried,
                query_piece,
                pair_piece[:, :HEAD_SIZE],
                pair_piece[:, HEAD_SIZE:],
                query_pos,
                query_start,
                key_pos,
            )

        half_rows = UNIT_TOKENS // 2

        def half_tile(carried, key_unit, pair_piece):
            key_pos = key_unit * UNIT_TOKENS + offsets
            part = tile_update(
                (carried[0][:, :half_rows], carried[1][:, :half_rows], carried[2][:half_rows]),
                query_piece[:half_rows],
                pair_piece[:, :HEAD_SIZE],
                pair_piece[:, HEAD_SIZE:],
                query_pos[:half_rows],
                query_start[:half_rows],
                key_pos,
            )
            return (
                lax.dynamic_update_slice_in_dim(carried[0], part[0], 0, 1),
                lax.dynamic_update_slice_in_dim(carried[1], part[1], 0, 1),
                lax.dynamic_update_slice_in_dim(carried[2], part[2], 0, 0),
            )

        def visit(step, carried):
            key_unit = position_unit - step
            key_row_unit = inverse[key_unit]
            source = (outer_index - key_row_unit // group_units) % outer_count
            key_row = (key_row_unit % group_units) * UNIT_TOKENS
            pair_piece = lax.switch(
                source,
                [
                    (lambda row, block=block: lax.dynamic_slice_in_dim(block, row, UNIT_TOKENS, 0))
                    for block in received
                ],
                key_row,
            )
            upper_needed = upper_start <= key_unit * UNIT_TOKENS + UNIT_TOKENS - 1
            return lax.cond(
                upper_needed,
                lambda c: tile_at(c, step, pair_piece),
                lambda c: half_tile(c, key_unit, pair_piece),
                carried,
            )

        running = (
            jnp.full((heads_here, UNIT_TOKENS), NEG_FILL, jnp.float32),
            jnp.zeros((heads_here, UNIT_TOKENS), jnp.float32),
            jnp.zeros((UNIT_TOKENS, heads_here, HEAD_SIZE), jnp.float32),
        )
        own_row = query_unit * UNIT_TOKENS
        running = tile_at(running, 0, own_pairs[own_row : own_row + UNIT_TOKENS])
        running, late_order, late_lengths = lax.optimization_barrier(
            (running, unit_order, doc_lengths)
        )
        inverse = jnp.zeros((unit_count,), jnp.int32).at[late_order].set(
            jnp.arange(unit_count, dtype=jnp.int32)
        )
        late_ends = jnp.cumsum(late_lengths).astype(jnp.int32)
        unit_start = jnp.max(
            jnp.where(late_ends <= late_order[group_begin + query_unit] * UNIT_TOKENS, late_ends, 0)
        )
        first_unit = unit_start // UNIT_TOKENS
        upper_pos = late_order[group_begin + query_unit] * UNIT_TOKENS + UNIT_TOKENS // 2
        upper_start = jnp.max(jnp.where(late_ends <= upper_pos, late_ends, 0))
        _, totals, accumulated = lax.fori_loop(
            1, position_unit - first_unit + 1, visit, running
        )
        outputs.append((accumulated, totals.T))
    accumulated = jnp.concatenate([part[0] for part in outputs], axis=0)
    totals = jnp.concatenate([part[1] for part in outputs], axis=0)

    def finished(chunk):
        begin = chunk * token_total
        rows = lax.dynamic_slice_in_dim(accumulated, begin, token_total, 0)
        sums = lax.dynamic_slice_in_dim(totals, begin, token_total, 0)
        return (rows / sums[:, :, None]).reshape(token_total, query_width).astype(jnp.bfloat16)

    return place_inner(finished, inner_index, inner_steps, query_width)


def solution(mesh):
    placed = (
        P(("outer", "inner"), None),
        P(("outer", "inner"), None),
        P(("outer", "inner"), None),
        P(),
        P(),
    )
    return jax.shard_map(
        body, mesh=mesh, in_specs=placed, out_specs=P(("outer", "inner"), None), check_vma=False
    )
```

```python
import jax
import jax.numpy as jnp
from jax import lax
from jax.sharding import PartitionSpec as P

QUERY_HEADS = 32
KEY_VALUE_HEADS = 4
HEAD_SIZE = 128
UNIT_TOKENS = 512


NEG_FILL = -1e30


def tile_update(running, query_piece, key_piece, value_piece, query_pos, query_start, key_pos):
    old_max, old_total, old_accum = running
    tile_rows, heads_here, _ = query_piece.shape
    allowed = (key_pos[None, :] >= query_start[:, None]) & (key_pos[None, :] <= query_pos[:, None])
    scores = jnp.einsum(
        "qhd,kd->hqk", query_piece, key_piece, preferred_element_type=jnp.float32
    ) * HEAD_SIZE ** (-0.5)
    scores = jnp.where(allowed[None], scores, NEG_FILL)
    new_max = jnp.maximum(old_max, jnp.max(scores, axis=2))
    weights = jnp.exp(scores - new_max[:, :, None])
    factor = jnp.exp(old_max - new_max)
    new_total = old_total * factor + jnp.sum(weights, axis=2)
    update = jnp.einsum(
        "hqk,kd->qhd",
        weights.astype(jnp.bfloat16),
        value_piece,
        preferred_element_type=jnp.float32,
    )
    new_accum = old_accum * factor.T[:, :, None] + update
    return (new_max, new_total, new_accum)


def swap_inner(piece_at, inner_index, inner_steps):
    arrived = [piece_at(inner_index)]
    for distance in range(1, inner_steps):
        route = [(i, (i + distance) % inner_steps) for i in range(inner_steps)]
        arrived.append(lax.ppermute(piece_at((inner_index + distance) % inner_steps), "inner", route))
    order = (inner_index - jnp.arange(inner_steps, dtype=jnp.int32)) % inner_steps
    return jnp.take(jnp.stack(arrived), order, axis=0)


def place_inner(piece_at, inner_index, inner_steps, width):
    arrived = [piece_at(inner_index)]
    for distance in range(1, inner_steps):
        route = [(i, (i + distance) % inner_steps) for i in range(inner_steps)]
        arrived.append(lax.ppermute(piece_at((inner_index + distance) % inner_steps), "inner", route))
    result = jnp.zeros((arrived[0].shape[0], inner_steps * width), arrived[0].dtype)
    for distance, piece in enumerate(arrived):
        column = ((inner_index - distance) % inner_steps) * width
        result = lax.dynamic_update_slice_in_dim(result, piece, column, 1)
    return result


def body(query_rows, key_matrix, value_matrix, unit_order, doc_lengths):
    inner_steps = lax.axis_size("inner")
    token_total = query_rows.shape[0]
    group_rows = inner_steps * token_total
    heads_here = QUERY_HEADS // inner_steps
    head_copies = inner_steps // KEY_VALUE_HEADS
    query_width = heads_here * HEAD_SIZE
    query_width = heads_here * HEAD_SIZE

    def widened_heads(score_matrix):
        return jnp.repeat(
            score_matrix.reshape(token_total, KEY_VALUE_HEADS, HEAD_SIZE), head_copies, axis=1
        )

    pairs = jnp.concatenate([widened_heads(key_matrix), widened_heads(value_matrix)], axis=2)
    inner_index = lax.axis_index("inner")
    pair_pieces = jnp.transpose(pairs, (1, 0, 2))
    own_pairs = swap_inner(
        lambda chunk: lax.dynamic_index_in_dim(pair_pieces, chunk, 0, keepdims=False),
        inner_index,
        inner_steps,
    )
    own_pairs = own_pairs.reshape(group_rows, 2 * HEAD_SIZE)
    outer_count = lax.axis_size("outer")
    outer_index = lax.axis_index("outer")
    received = [own_pairs]
    for distance in range(1, outer_count):
        route = [(i, (i + distance) % outer_count) for i in range(outer_count)]
        received.append(lax.ppermute(own_pairs, "outer", route))
    local_queries = lax.all_to_all(query_rows, "inner", split_axis=1, concat_axis=0, tiled=True)
    local_queries, early_order, early_lengths = lax.optimization_barrier(
        (local_queries, unit_order, doc_lengths)
    )
    shaped_queries = local_queries.reshape(group_rows, heads_here, HEAD_SIZE)
    unit_count = unit_order.shape[0]
    group_units = group_rows // UNIT_TOKENS
    group_begin = outer_index * group_units
    offsets = jnp.arange(UNIT_TOKENS, dtype=jnp.int32)
    early_ends = jnp.cumsum(early_lengths).astype(jnp.int32)

    outputs = []
    for query_unit in range(group_units):
        position_unit = early_order[group_begin + query_unit]
        query_pos = position_unit * UNIT_TOKENS + offsets
        query_start = jnp.max(
            jnp.where(early_ends[None, :] <= query_pos[:, None], early_ends[None, :], 0), axis=1
        )
        query_piece = shaped_queries[query_unit * UNIT_TOKENS : (query_unit + 1) * UNIT_TOKENS]

        def tile_at(carried, step, pair_piece):
            key_unit = position_unit - step
            key_pos = key_unit * UNIT_TOKENS + offsets
            return tile_update(
                carried,
                query_piece,
                pair_piece[:, :HEAD_SIZE],
                pair_piece[:, HEAD_SIZE:],
                query_pos,
                query_start,
                key_pos,
            )

        def visit(step, carried):
            key_row_unit = inverse[position_unit - step]
            source = (outer_index - key_row_unit // group_units) % outer_count
            key_row = (key_row_unit % group_units) * UNIT_TOKENS
            pair_piece = lax.switch(
                source,
                [
                    (lambda row, block=block: lax.dynamic_slice_in_dim(block, row, UNIT_TOKENS, 0))
                    for block in received
                ],
                key_row,
            )
            return tile_at(carried, step, pair_piece)

        running = (
            jnp.full((heads_here, UNIT_TOKENS), NEG_FILL, jnp.float32),
            jnp.zeros((heads_here, UNIT_TOKENS), jnp.float32),
            jnp.zeros((UNIT_TOKENS, heads_here, HEAD_SIZE), jnp.float32),
        )
        own_row = query_unit * UNIT_TOKENS
        running = tile_at(running, 0, own_pairs[own_row : own_row + UNIT_TOKENS])
        running, late_order, late_lengths = lax.optimization_barrier(
            (running, unit_order, doc_lengths)
        )
        inverse = jnp.zeros((unit_count,), jnp.int32).at[late_order].set(
            jnp.arange(unit_count, dtype=jnp.int32)
        )
        late_ends = jnp.cumsum(late_lengths).astype(jnp.int32)
        unit_start = jnp.max(
            jnp.where(late_ends <= late_order[group_begin + query_unit] * UNIT_TOKENS, late_ends, 0)
        )
        first_unit = unit_start // UNIT_TOKENS
        _, totals, accumulated = lax.fori_loop(
            1, position_unit - first_unit + 1, visit, running
        )
        outputs.append((accumulated, totals.T))
    accumulated = jnp.concatenate([part[0] for part in outputs], axis=0)
    totals = jnp.concatenate([part[1] for part in outputs], axis=0)

    def finished(chunk):
        begin = chunk * token_total
        rows = lax.dynamic_slice_in_dim(accumulated, begin, token_total, 0)
        sums = lax.dynamic_slice_in_dim(totals, begin, token_total, 0)
        return (rows / sums[:, :, None]).reshape(token_total, query_width).astype(jnp.bfloat16)

    return place_inner(finished, inner_index, inner_steps, query_width)


def solution(mesh):
    placed = (
        P(("outer", "inner"), None),
        P(("outer", "inner"), None),
        P(("outer", "inner"), None),
        P(),
        P(),
    )
    return jax.shard_map(
        body, mesh=mesh, in_specs=placed, out_specs=P(("outer", "inner"), None), check_vma=False
    )
```

```python
import jax
import jax.numpy as jnp
from jax import lax
from jax.sharding import PartitionSpec as P

QUERY_HEADS = 32
KEY_VALUE_HEADS = 4
HEAD_SIZE = 128
UNIT_TOKENS = 512


NEG_FILL = -1e30


def tile_update(running, query_piece, key_piece, value_piece, query_pos, query_start, key_pos):
    old_max, old_total, old_accum = running
    tile_rows, heads_here, _ = query_piece.shape
    allowed = (key_pos[None, :] >= query_start[:, None]) & (key_pos[None, :] <= query_pos[:, None])
    scores = jnp.einsum(
        "qhd,kd->hqk", query_piece, key_piece, preferred_element_type=jnp.float32
    ) * HEAD_SIZE ** (-0.5)
    scores = jnp.where(allowed[None], scores, NEG_FILL)
    new_max = jnp.maximum(old_max, jnp.max(scores, axis=2))
    weights = jnp.where(allowed[None], jnp.exp(scores - new_max[:, :, None]), 0.0)
    factor = jnp.exp(old_max - new_max)
    new_total = old_total * factor + jnp.sum(weights, axis=2)
    update = jnp.einsum(
        "hqk,kd->qhd",
        weights.astype(jnp.bfloat16),
        value_piece,
        preferred_element_type=jnp.float32,
    )
    new_accum = old_accum * factor.T[:, :, None] + update
    return (new_max, new_total, new_accum)


def swap_inner(piece_at, inner_index, inner_steps):
    arrived = [piece_at(inner_index)]
    for distance in range(1, inner_steps):
        route = [(i, (i + distance) % inner_steps) for i in range(inner_steps)]
        arrived.append(lax.ppermute(piece_at((inner_index + distance) % inner_steps), "inner", route))
    order = (inner_index - jnp.arange(inner_steps, dtype=jnp.int32)) % inner_steps
    return jnp.take(jnp.stack(arrived), order, axis=0)


def place_inner(piece_at, inner_index, inner_steps, width):
    arrived = [piece_at(inner_index)]
    for distance in range(1, inner_steps):
        route = [(i, (i + distance) % inner_steps) for i in range(inner_steps)]
        arrived.append(lax.ppermute(piece_at((inner_index + distance) % inner_steps), "inner", route))
    result = jnp.zeros((arrived[0].shape[0], inner_steps * width), arrived[0].dtype)
    for distance, piece in enumerate(arrived):
        column = ((inner_index - distance) % inner_steps) * width
        result = lax.dynamic_update_slice_in_dim(result, piece, column, 1)
    return result


def body(query_rows, key_matrix, value_matrix, unit_order, doc_lengths):
    inner_steps = lax.axis_size("inner")
    token_total = query_rows.shape[0]
    group_rows = inner_steps * token_total
    heads_here = QUERY_HEADS // inner_steps
    head_copies = inner_steps // KEY_VALUE_HEADS
    query_width = heads_here * HEAD_SIZE
    query_width = heads_here * HEAD_SIZE

    def widened_heads(score_matrix):
        return jnp.repeat(
            score_matrix.reshape(token_total, KEY_VALUE_HEADS, HEAD_SIZE), head_copies, axis=1
        )

    pairs = jnp.concatenate([widened_heads(key_matrix), widened_heads(value_matrix)], axis=2)
    inner_index = lax.axis_index("inner")
    pair_pieces = jnp.transpose(pairs, (1, 0, 2))
    own_pairs = swap_inner(
        lambda chunk: lax.dynamic_index_in_dim(pair_pieces, chunk, 0, keepdims=False),
        inner_index,
        inner_steps,
    )
    own_pairs = own_pairs.reshape(group_rows, 2 * HEAD_SIZE)
    outer_count = lax.axis_size("outer")
    outer_index = lax.axis_index("outer")
    minor = 2 if outer_count % 2 == 0 else 1
    major = outer_count // minor
    along_major = [own_pairs]
    for distance in range(1, major):
        route = [
            (i, ((i // minor + distance) % major) * minor + i % minor) for i in range(outer_count)
        ]
        along_major.append(lax.ppermute(own_pairs, "outer", route))
    received = []
    for block in along_major:
        received.append(block)
        for flip in range(1, minor):
            route = [(i, (i // minor) * minor + (i % minor + flip) % minor) for i in range(outer_count)]
            received.append(lax.ppermute(block, "outer", route))
    local_queries = lax.all_to_all(query_rows, "inner", split_axis=1, concat_axis=0, tiled=True)
    local_queries, early_order, early_lengths = lax.optimization_barrier(
        (local_queries, unit_order, doc_lengths)
    )
    shaped_queries = local_queries.reshape(group_rows, heads_here, HEAD_SIZE)
    unit_count = unit_order.shape[0]
    group_units = group_rows // UNIT_TOKENS
    group_begin = outer_index * group_units
    offsets = jnp.arange(UNIT_TOKENS, dtype=jnp.int32)
    early_ends = jnp.cumsum(early_lengths).astype(jnp.int32)

    outputs = []
    for query_unit in range(group_units):
        position_unit = early_order[group_begin + query_unit]
        query_pos = position_unit * UNIT_TOKENS + offsets
        query_start = jnp.max(
            jnp.where(early_ends[None, :] <= query_pos[:, None], early_ends[None, :], 0), axis=1
        )
        query_piece = shaped_queries[query_unit * UNIT_TOKENS : (query_unit + 1) * UNIT_TOKENS]

        def tile_at(carried, step, pair_piece):
            key_unit = position_unit - step
            key_pos = key_unit * UNIT_TOKENS + offsets
            return tile_update(
                carried,
                query_piece,
                pair_piece[:, :HEAD_SIZE],
                pair_piece[:, HEAD_SIZE:],
                query_pos,
                query_start,
                key_pos,
            )

        def visit(step, carried):
            key_row_unit = inverse[position_unit - step]
            key_group = key_row_unit // group_units
            source = ((outer_index // minor - key_group // minor) % major) * minor + (
                outer_index % minor - key_group % minor
            ) % minor
            key_row = (key_row_unit % group_units) * UNIT_TOKENS
            pair_piece = lax.switch(
                source,
                [
                    (lambda row, block=block: lax.dynamic_slice_in_dim(block, row, UNIT_TOKENS, 0))
                    for block in received
                ],
                key_row,
            )
            return tile_at(carried, step, pair_piece)

        running = (
            jnp.full((heads_here, UNIT_TOKENS), NEG_FILL, jnp.float32),
            jnp.zeros((heads_here, UNIT_TOKENS), jnp.float32),
            jnp.zeros((UNIT_TOKENS, heads_here, HEAD_SIZE), jnp.float32),
        )
        own_row = query_unit * UNIT_TOKENS
        running = tile_at(running, 0, own_pairs[own_row : own_row + UNIT_TOKENS])
        running, late_order, late_lengths = lax.optimization_barrier(
            (running, unit_order, doc_lengths)
        )
        inverse = jnp.zeros((unit_count,), jnp.int32).at[late_order].set(
            jnp.arange(unit_count, dtype=jnp.int32)
        )
        late_ends = jnp.cumsum(late_lengths).astype(jnp.int32)
        unit_start = jnp.max(
            jnp.where(late_ends <= late_order[group_begin + query_unit] * UNIT_TOKENS, late_ends, 0)
        )
        first_unit = unit_start // UNIT_TOKENS
        _, totals, accumulated = lax.fori_loop(
            1, position_unit - first_unit + 1, visit, running
        )
        outputs.append((accumulated, totals.T))
    accumulated = jnp.concatenate([part[0] for part in outputs], axis=0)
    totals = jnp.concatenate([part[1] for part in outputs], axis=0)

    def finished(chunk):
        begin = chunk * token_total
        rows = lax.dynamic_slice_in_dim(accumulated, begin, token_total, 0)
        sums = lax.dynamic_slice_in_dim(totals, begin, token_total, 0)
        return (rows / sums[:, :, None]).reshape(token_total, query_width).astype(jnp.bfloat16)

    return place_inner(finished, inner_index, inner_steps, query_width)


def solution(mesh):
    placed = (
        P(("outer", "inner"), None),
        P(("outer", "inner"), None),
        P(("outer", "inner"), None),
        P(),
        P(),
    )
    return jax.shard_map(
        body, mesh=mesh, in_specs=placed, out_specs=P(("outer", "inner"), None), check_vma=False
    )
```

```python
import jax
import jax.numpy as jnp
from jax import lax
from jax.sharding import PartitionSpec as P

QUERY_HEADS = 32
KEY_VALUE_HEADS = 4
HEAD_SIZE = 128
UNIT_TOKENS = 512


NEG_FILL = -1e30


def tile_update(running, query_piece, key_piece, value_piece, query_pos, query_start, key_pos):
    old_max, old_total, old_accum = running
    tile_rows, heads_here, _ = query_piece.shape
    allowed = (key_pos[None, :] >= query_start[:, None]) & (key_pos[None, :] <= query_pos[:, None])
    scores = jnp.einsum(
        "qhd,kd->hqk", query_piece, key_piece, preferred_element_type=jnp.float32
    ) * HEAD_SIZE ** (-0.5)
    scores = jnp.where(allowed[None], scores, NEG_FILL)
    new_max = jnp.maximum(old_max, jnp.max(scores, axis=2))
    weights = jnp.where(allowed[None], jnp.exp(scores - new_max[:, :, None]), 0.0)
    factor = jnp.exp(old_max - new_max)
    new_total = old_total * factor + jnp.sum(weights, axis=2)
    update = jnp.einsum(
        "hqk,kd->qhd",
        weights.astype(jnp.bfloat16),
        value_piece,
        preferred_element_type=jnp.float32,
    )
    new_accum = old_accum * factor.T[:, :, None] + update
    return (new_max, new_total, new_accum)


def swap_inner(piece_at, inner_index, inner_steps):
    arrived = [piece_at(inner_index)]
    for distance in range(1, inner_steps):
        route = [(i, (i + distance) % inner_steps) for i in range(inner_steps)]
        arrived.append(lax.ppermute(piece_at((inner_index + distance) % inner_steps), "inner", route))
    order = (inner_index - jnp.arange(inner_steps, dtype=jnp.int32)) % inner_steps
    return jnp.take(jnp.stack(arrived), order, axis=0)


def place_inner(piece_at, inner_index, inner_steps, width):
    arrived = [piece_at(inner_index)]
    for distance in range(1, inner_steps):
        route = [(i, (i + distance) % inner_steps) for i in range(inner_steps)]
        arrived.append(lax.ppermute(piece_at((inner_index + distance) % inner_steps), "inner", route))
    result = jnp.zeros((arrived[0].shape[0], inner_steps * width), arrived[0].dtype)
    for distance, piece in enumerate(arrived):
        column = ((inner_index - distance) % inner_steps) * width
        result = lax.dynamic_update_slice_in_dim(result, piece, column, 1)
    return result


def body(query_rows, key_matrix, value_matrix, unit_order, doc_lengths):
    inner_steps = lax.axis_size("inner")
    token_total = query_rows.shape[0]
    group_rows = inner_steps * token_total
    heads_here = QUERY_HEADS // inner_steps
    head_copies = inner_steps // KEY_VALUE_HEADS
    query_width = heads_here * HEAD_SIZE
    query_width = heads_here * HEAD_SIZE

    def widened_heads(score_matrix):
        return jnp.repeat(
            score_matrix.reshape(token_total, KEY_VALUE_HEADS, HEAD_SIZE), head_copies, axis=1
        )

    pairs = jnp.concatenate([widened_heads(key_matrix), widened_heads(value_matrix)], axis=2)
    inner_index = lax.axis_index("inner")
    pair_pieces = jnp.transpose(pairs, (1, 0, 2))
    own_pairs = swap_inner(
        lambda chunk: lax.dynamic_index_in_dim(pair_pieces, chunk, 0, keepdims=False),
        inner_index,
        inner_steps,
    )
    own_pairs = own_pairs.reshape(group_rows, 2 * HEAD_SIZE)
    outer_count = lax.axis_size("outer")
    outer_index = lax.axis_index("outer")
    minor = 2 if outer_count % 2 == 0 else 1
    major = outer_count // minor
    along_major = [own_pairs]
    for distance in range(1, major):
        route = [
            (i, ((i // minor + distance) % major) * minor + i % minor) for i in range(outer_count)
        ]
        along_major.append(lax.ppermute(own_pairs, "outer", route))
    received = []
    for block in along_major:
        received.append(block)
        for flip in range(1, minor):
            route = [(i, (i // minor) * minor + (i % minor + flip) % minor) for i in range(outer_count)]
            received.append(lax.ppermute(block, "outer", route))
    local_queries = lax.all_to_all(query_rows, "inner", split_axis=1, concat_axis=0, tiled=True)
    local_queries, early_order, early_lengths = lax.optimization_barrier(
        (local_queries, unit_order, doc_lengths)
    )
    shaped_queries = local_queries.reshape(group_rows, heads_here, HEAD_SIZE)
    unit_count = unit_order.shape[0]
    group_units = group_rows // UNIT_TOKENS
    group_begin = outer_index * group_units
    offsets = jnp.arange(UNIT_TOKENS, dtype=jnp.int32)
    early_ends = jnp.cumsum(early_lengths).astype(jnp.int32)

    outputs = []
    for query_unit in range(group_units):
        position_unit = early_order[group_begin + query_unit]
        query_pos = position_unit * UNIT_TOKENS + offsets
        query_start = jnp.max(
            jnp.where(early_ends[None, :] <= query_pos[:, None], early_ends[None, :], 0), axis=1
        )
        query_piece = shaped_queries[query_unit * UNIT_TOKENS : (query_unit + 1) * UNIT_TOKENS]

        def tile_at(carried, step, pair_piece):
            key_unit = position_unit - step
            key_pos = key_unit * UNIT_TOKENS + offsets
            return tile_update(
                carried,
                query_piece,
                pair_piece[:, :HEAD_SIZE],
                pair_piece[:, HEAD_SIZE:],
                query_pos,
                query_start,
                key_pos,
            )

        def visit(step, carried):
            key_row_unit = inverse[position_unit - step]
            key_group = key_row_unit // group_units
            source = ((outer_index // minor - key_group // minor) % major) * minor + (
                outer_index % minor - key_group % minor
            ) % minor
            key_row = (key_row_unit % group_units) * UNIT_TOKENS
            pair_piece = lax.switch(
                source,
                [
                    (lambda row, block=block: lax.dynamic_slice_in_dim(block, row, UNIT_TOKENS, 0))
                    for block in received
                ],
                key_row,
            )
            return tile_at(carried, step, pair_piece)

        running = (
            jnp.full((heads_here, UNIT_TOKENS), NEG_FILL, jnp.float32),
            jnp.zeros((heads_here, UNIT_TOKENS), jnp.float32),
            jnp.zeros((UNIT_TOKENS, heads_here, HEAD_SIZE), jnp.float32),
        )
        own_row = query_unit * UNIT_TOKENS
        running = tile_at(running, 0, own_pairs[own_row : own_row + UNIT_TOKENS])
        _, late_order, late_lengths = lax.optimization_barrier(
            (received[minor % len(received)], unit_order, doc_lengths)
        )
        inverse = jnp.zeros((unit_count,), jnp.int32).at[late_order].set(
            jnp.arange(unit_count, dtype=jnp.int32)
        )
        late_ends = jnp.cumsum(late_lengths).astype(jnp.int32)
        unit_start = jnp.max(
            jnp.where(late_ends <= late_order[group_begin + query_unit] * UNIT_TOKENS, late_ends, 0)
        )
        first_unit = unit_start // UNIT_TOKENS
        _, totals, accumulated = lax.fori_loop(
            1, position_unit - first_unit + 1, visit, running
        )
        outputs.append((accumulated, totals.T))
    accumulated = jnp.concatenate([part[0] for part in outputs], axis=0)
    totals = jnp.concatenate([part[1] for part in outputs], axis=0)

    def finished(chunk):
        begin = chunk * token_total
        rows = lax.dynamic_slice_in_dim(accumulated, begin, token_total, 0)
        sums = lax.dynamic_slice_in_dim(totals, begin, token_total, 0)
        return (rows / sums[:, :, None]).reshape(token_total, query_width).astype(jnp.bfloat16)

    return place_inner(finished, inner_index, inner_steps, query_width)


def solution(mesh):
    placed = (
        P(("outer", "inner"), None),
        P(("outer", "inner"), None),
        P(("outer", "inner"), None),
        P(),
        P(),
    )
    return jax.shard_map(
        body, mesh=mesh, in_specs=placed, out_specs=P(("outer", "inner"), None), check_vma=False
    )
```

```python
import jax
import jax.numpy as jnp
from jax import lax
from jax.sharding import PartitionSpec as P

QUERY_HEADS = 32
KEY_VALUE_HEADS = 4
HEAD_SIZE = 128
UNIT_TOKENS = 512


NEG_FILL = -1e30


def tile_update(running, query_piece, key_piece, value_piece, query_pos, query_start, key_pos):
    old_max, old_total, old_accum = running
    tile_rows, heads_here, _ = query_piece.shape
    allowed = (key_pos[None, :] >= query_start[:, None]) & (key_pos[None, :] <= query_pos[:, None])
    scores = jnp.einsum(
        "qhd,kd->hqk", query_piece, key_piece, preferred_element_type=jnp.float32
    ) * HEAD_SIZE ** (-0.5)
    scores = jnp.where(allowed[None], scores, NEG_FILL)
    new_max = jnp.maximum(old_max, jnp.max(scores, axis=2))
    weights = jnp.where(allowed[None], jnp.exp(scores - new_max[:, :, None]), 0.0)
    factor = jnp.exp(old_max - new_max)
    new_total = old_total * factor + jnp.sum(weights, axis=2)
    update = jnp.einsum(
        "hqk,kd->qhd",
        weights.astype(jnp.bfloat16),
        value_piece,
        preferred_element_type=jnp.float32,
    )
    new_accum = old_accum * factor.T[:, :, None] + update
    return (new_max, new_total, new_accum)


def swap_inner(piece_at, inner_index, inner_steps):
    arrived = [piece_at(inner_index)]
    for distance in range(1, inner_steps):
        route = [(i, (i + distance) % inner_steps) for i in range(inner_steps)]
        arrived.append(lax.ppermute(piece_at((inner_index + distance) % inner_steps), "inner", route))
    order = (inner_index - jnp.arange(inner_steps, dtype=jnp.int32)) % inner_steps
    return jnp.take(jnp.stack(arrived), order, axis=0)


def place_inner(piece_at, inner_index, inner_steps, width):
    arrived = [piece_at(inner_index)]
    for distance in range(1, inner_steps):
        route = [(i, (i + distance) % inner_steps) for i in range(inner_steps)]
        arrived.append(lax.ppermute(piece_at((inner_index + distance) % inner_steps), "inner", route))
    result = jnp.zeros((arrived[0].shape[0], inner_steps * width), arrived[0].dtype)
    for distance, piece in enumerate(arrived):
        column = ((inner_index - distance) % inner_steps) * width
        result = lax.dynamic_update_slice_in_dim(result, piece, column, 1)
    return result


def body(query_rows, key_matrix, value_matrix, unit_order, doc_lengths):
    inner_steps = lax.axis_size("inner")
    token_total = query_rows.shape[0]
    group_rows = inner_steps * token_total
    heads_here = QUERY_HEADS // inner_steps
    head_copies = inner_steps // KEY_VALUE_HEADS
    query_width = heads_here * HEAD_SIZE
    query_width = heads_here * HEAD_SIZE

    def widened_heads(score_matrix):
        return jnp.repeat(
            score_matrix.reshape(token_total, KEY_VALUE_HEADS, HEAD_SIZE), head_copies, axis=1
        )

    pairs = jnp.concatenate([widened_heads(key_matrix), widened_heads(value_matrix)], axis=2)
    inner_index = lax.axis_index("inner")
    pair_pieces = jnp.transpose(pairs, (1, 0, 2))
    own_pairs = swap_inner(
        lambda chunk: lax.dynamic_index_in_dim(pair_pieces, chunk, 0, keepdims=False),
        inner_index,
        inner_steps,
    )
    own_pairs = own_pairs.reshape(group_rows, 2 * HEAD_SIZE)
    outer_count = lax.axis_size("outer")
    outer_index = lax.axis_index("outer")
    minor = 2 if outer_count % 2 == 0 else 1
    major = outer_count // minor
    along_major = [own_pairs]
    for distance in range(1, major):
        route = [
            (i, ((i // minor + distance) % major) * minor + i % minor) for i in range(outer_count)
        ]
        along_major.append(lax.ppermute(own_pairs, "outer", route))
    received = []
    for block in along_major:
        received.append(block)
        for flip in range(1, minor):
            route = [(i, (i // minor) * minor + (i % minor + flip) % minor) for i in range(outer_count)]
            received.append(lax.ppermute(block, "outer", route))
    local_queries = lax.all_to_all(query_rows, "inner", split_axis=1, concat_axis=0, tiled=True)
    _, early_order, early_lengths = lax.optimization_barrier(
        (received[minor % len(received)], unit_order, doc_lengths)
    )
    shaped_queries = local_queries.reshape(group_rows, heads_here, HEAD_SIZE)
    unit_count = unit_order.shape[0]
    group_units = group_rows // UNIT_TOKENS
    group_begin = outer_index * group_units
    offsets = jnp.arange(UNIT_TOKENS, dtype=jnp.int32)
    early_ends = jnp.cumsum(early_lengths).astype(jnp.int32)

    outputs = []
    for query_unit in range(group_units):
        position_unit = early_order[group_begin + query_unit]
        query_pos = position_unit * UNIT_TOKENS + offsets
        query_start = jnp.max(
            jnp.where(early_ends[None, :] <= query_pos[:, None], early_ends[None, :], 0), axis=1
        )
        query_piece = shaped_queries[query_unit * UNIT_TOKENS : (query_unit + 1) * UNIT_TOKENS]

        def tile_at(carried, step, pair_piece):
            key_unit = position_unit - step
            key_pos = key_unit * UNIT_TOKENS + offsets
            return tile_update(
                carried,
                query_piece,
                pair_piece[:, :HEAD_SIZE],
                pair_piece[:, HEAD_SIZE:],
                query_pos,
                query_start,
                key_pos,
            )

        def visit(step, carried):
            key_row_unit = inverse[position_unit - step]
            key_group = key_row_unit // group_units
            source = ((outer_index // minor - key_group // minor) % major) * minor + (
                outer_index % minor - key_group % minor
            ) % minor
            key_row = (key_row_unit % group_units) * UNIT_TOKENS
            pair_piece = lax.switch(
                source,
                [
                    (lambda row, block=block: lax.dynamic_slice_in_dim(block, row, UNIT_TOKENS, 0))
                    for block in received
                ],
                key_row,
            )
            return tile_at(carried, step, pair_piece)

        running = (
            jnp.full((heads_here, UNIT_TOKENS), NEG_FILL, jnp.float32),
            jnp.zeros((heads_here, UNIT_TOKENS), jnp.float32),
            jnp.zeros((UNIT_TOKENS, heads_here, HEAD_SIZE), jnp.float32),
        )
        own_row = query_unit * UNIT_TOKENS
        running = tile_at(running, 0, own_pairs[own_row : own_row + UNIT_TOKENS])
        _, late_order, late_lengths = lax.optimization_barrier(
            (received[minor % len(received)], unit_order, doc_lengths)
        )
        inverse = jnp.zeros((unit_count,), jnp.int32).at[late_order].set(
            jnp.arange(unit_count, dtype=jnp.int32)
        )
        late_ends = jnp.cumsum(late_lengths).astype(jnp.int32)
        unit_start = jnp.max(
            jnp.where(late_ends <= late_order[group_begin + query_unit] * UNIT_TOKENS, late_ends, 0)
        )
        first_unit = unit_start // UNIT_TOKENS
        _, totals, accumulated = lax.fori_loop(
            1, position_unit - first_unit + 1, visit, running
        )
        outputs.append((accumulated, totals.T))
    accumulated = jnp.concatenate([part[0] for part in outputs], axis=0)
    totals = jnp.concatenate([part[1] for part in outputs], axis=0)

    def finished(chunk):
        begin = chunk * token_total
        rows = lax.dynamic_slice_in_dim(accumulated, begin, token_total, 0)
        sums = lax.dynamic_slice_in_dim(totals, begin, token_total, 0)
        return (rows / sums[:, :, None]).reshape(token_total, query_width).astype(jnp.bfloat16)

    return place_inner(finished, inner_index, inner_steps, query_width)


def solution(mesh):
    placed = (
        P(("outer", "inner"), None),
        P(("outer", "inner"), None),
        P(("outer", "inner"), None),
        P(),
        P(),
    )
    return jax.shard_map(
        body, mesh=mesh, in_specs=placed, out_specs=P(("outer", "inner"), None), check_vma=False
    )
```
